32 devices in a mesh: row: 8 (over y, x, core), col: 4 (over z).
Axes of the slice: x: 2, y: 2, z: 4, core: 2. Of those that a mesh axis runs over, the one named last changes fastest.
Arguments:
- out_grads: bfloat16 [64, 28672], P('col', 'row'), may hold values from -6 to 6
- in_acts: bfloat16 [64, 8192], P('row', 'col'), may hold values from -6 to 6
- out_basis: bfloat16 [28672, 28672], P('row', 'col'), may hold values from -0.03125 to 0.03125
- in_basis: bfloat16 [8192, 8192], P('col', 'row'), may hold values from -0.0625 to 0.0625
- eigenvalues: bfloat16 [28672, 8192], P('col', 'row'), may hold values from 0.019897461 to 2
- queries: bfloat16 [2, 28672, 8192], P(None, 'col', 'row'), may hold values from -0.00015640259 to 0.00015640259
Outputs:
- scores: float32 [2, 64], replicated
The draws below stay inside these ranges and needn't reach their ends.
All inputs are finite; a program needn't handle non-finite values.
Results may differ from the reference program's by a relative error of at most 0.0045.
Values may be sent and summed in bfloat16 or wider, within the bound.
No kernel may reach another device: no remote copies, remote signals or barrier semaphores. Data moves between devices by JAX's collectives and lax.ppermute only.
A program may use at most 192 MiB of HBM per device.

```python
import math
import jax
import jax.numpy as jnp
from jax import lax

D_IN = 8192
D_OUT = 28672
QUERIES = 2
TOKENS = 64


def block_scale(rng, dims, split, least, top_value):
    gain = 1.0
    for axis_at, blocks in split:
        heights = jax.random.uniform(jax.random.fold_in(jax.random.fold_in(rng, 6), axis_at), (blocks,), jnp.float32, least / len(split), top_value / len(split))
        gain = gain * jnp.repeat(jnp.exp(heights), dims[axis_at] // blocks).reshape((-1,) + (1,) * (len(dims) - 1 - axis_at))
    return gain


def scatter_about(key, extent, deviation, bound, cuts=(), kind=jnp.bfloat16):
    level = block_scale(key, extent, cuts, -0.22, 0.18) if cuts else 1.0
    drawn = jax.random.normal(key, extent, jnp.float32) * deviation * level
    return jnp.minimum(jnp.maximum(drawn, -bound), bound).astype(kind)


def setup_inputs(seed: int = 0) -> dict:
    key_list = jax.random.split(jax.random.key(seed), 7)
    out_grads = scatter_about(key_list[0], (TOKENS, D_OUT), 1.0, 6.0, ((0, 4), (1, 8)))
    in_acts = scatter_about(key_list[1], (TOKENS, D_IN), 1.0, 6.0, ((0, 8), (1, 4)))
    out_basis = scatter_about(key_list[2], (D_OUT, D_OUT), D_OUT ** -0.5, 0.03125, ((0, 8), (1, 4)))
    in_basis = scatter_about(key_list[3], (D_IN, D_IN), D_IN ** -0.5, 0.0625, ((0, 4), (1, 8)))
    eigenvalues = jnp.clip(jnp.exp(math.log(2.0) - 4.61031033 * jax.random.uniform(key_list[4], (D_OUT, D_IN), jnp.float32) ** block_scale(key_list[4], (D_OUT, D_IN), ((0, 4), (1, 8)), -0.2, 0.2)), 0.019897461, 2.0).astype(jnp.bfloat16)
    queries = scatter_about(key_list[5], (QUERIES, D_OUT, D_IN), (0.4 / (D_IN * D_OUT) ** 0.5), 0.00015640259, ((1, 4), (2, 8)))
    return dict(out_grads=out_grads, in_acts=in_acts, out_basis=out_basis, in_basis=in_basis, eigenvalues=eigenvalues, queries=queries)


DAMPING = 0.1


def reference(out_grads, in_acts, out_basis, in_basis, eigenvalues, queries):
    grad_rot = jnp.dot(out_grads, out_basis, preferred_element_type=jnp.float32).astype(jnp.bfloat16)
    act_rot = jnp.dot(in_acts, in_basis, preferred_element_type=jnp.float32).astype(jnp.bfloat16)
    grad_wide = grad_rot.astype(jnp.float32)
    act_wide = act_rot.astype(jnp.float32)
    shifted = eigenvalues.astype(jnp.float32) + DAMPING

    def one_query(query):
        scaled = query.astype(jnp.float32) / shifted
        lifted = jnp.dot(scaled, act_wide.T, precision=lax.Precision.HIGHEST, preferred_element_type=jnp.float32)
        return jnp.sum(lifted * grad_wide.T, axis=0)

    return lax.map(one_query, queries)
```

```python
import functools

import jax
import jax.numpy as jnp
from jax import lax
from jax.experimental import pallas as pl
from jax.experimental.pallas import tpu as pltpu
from jax.sharding import PartitionSpec as P

DAMPING = 0.1
F32 = jnp.float32
BF16 = jnp.bfloat16


def _swap(x, axis, n, b):
    return lax.ppermute(x, axis, [(i, i ^ b) for i in range(n)])


def _gather(x, axis, n, dim):
    me = lax.axis_index(axis)
    b = 1
    while b < n:
        other = _swap(x, axis, n, b)
        first = (me // b) % 2 == 0
        x = jnp.where(first, jnp.concatenate([x, other], dim), jnp.concatenate([other, x], dim))
        b *= 2
    return x


def _allreduce_bf16(x, axis, n, dim):
    me = lax.axis_index(axis)
    b = 1
    while b < n:
        half = x.shape[dim] // 2
        upper = (me // b) % 2 == 1
        lo = lax.slice_in_dim(x, 0, half, axis=dim)
        hi = lax.slice_in_dim(x, half, 2 * half, axis=dim)
        keep = jnp.where(upper, hi, lo)
        send = jnp.where(upper, lo, hi)
        x = keep + _swap(send, axis, n, b)
        b *= 2
    x = x.astype(BF16)
    b = n // 2
    while b >= 1:
        other = _swap(x, axis, n, b)
        first = (me // b) % 2 == 0
        x = jnp.where(first, jnp.concatenate([x, other], dim), jnp.concatenate([other, x], dim))
        b //= 2
    return x


def _allreduce_small(x, axis, n):
    b = 1
    while b < n:
        x = x + _swap(x, axis, n, b)
        b *= 2
    return x


def _lifted_kernel(a_ref, e_ref, q_ref, o_ref):
    recip = 1.0 / (e_ref[...].astype(F32) + DAMPING)
    a = a_ref[...]
    dims = (((1,), (1,)), ((), ()))
    for qi in range(q_ref.shape[0]):
        s = q_ref[qi].astype(F32) * recip
        hi = s.astype(BF16)
        lo = (s - hi.astype(F32)).astype(BF16)
        o_ref[qi] = lax.dot_general(a, hi, dims, preferred_element_type=F32) + lax.dot_general(
            a, lo, dims, preferred_element_type=F32
        )


def _lifted(act_rot, eigenvalues, queries):
    nq, kk, jj = queries.shape
    tt = act_rot.shape[0]
    tk = next(c for c in (512, 256, 128, kk) if kk % c == 0)
    return pl.pallas_call(
        _lifted_kernel,
        grid=(kk // tk,),
        in_specs=[
            pl.BlockSpec((tt, jj), lambda i: (0, 0)),
            pl.BlockSpec((tk, jj), lambda i: (i, 0)),
            pl.BlockSpec((nq, tk, jj), lambda i: (0, i, 0)),
        ],
        out_specs=pl.BlockSpec((nq, tt, tk), lambda i: (0, 0, i)),
        out_shape=jax.ShapeDtypeStruct((nq, tt, kk), F32),
        compiler_params=pltpu.CompilerParams(dimension_semantics=("arbitrary",)),
        cost_estimate=pl.CostEstimate(
            flops=4 * nq * kk * jj * tt,
            bytes_accessed=(nq + 1) * kk * jj * 2 + nq * tt * kk * 4,
            transcendentals=0,
        ),
    )(act_rot, eigenvalues, queries)


def local(out_grads, in_acts, out_basis, in_basis, eigenvalues, queries, *, nr, nc):
    acts_all = _gather(in_acts, "row", nr, 0)
    grads_all = _gather(out_grads, "col", nc, 0)
    act_part = jnp.dot(acts_all, in_basis, preferred_element_type=F32)
    act_rot = _allreduce_bf16(act_part, "col", nc, 1)
    grad_part = jnp.dot(grads_all, out_basis, preferred_element_type=F32)
    grad_rot = _allreduce_bf16(grad_part, "row", nr, 1)
    lifted = _lifted(act_rot, eigenvalues, queries)
    partial = jnp.sum(lifted * grad_rot.astype(F32)[None], axis=2)
    return _allreduce_small(_allreduce_small(partial, "col", nc), "row", nr)


def solution(mesh):
    in_specs = (
        P("col", "row"),
        P("row", "col"),
        P("row", "col"),
        P("col", "row"),
        P("col", "row"),
        P(None, "col", "row"),
    )
    fn = functools.partial(local, nr=mesh.shape["row"], nc=mesh.shape["col"])
    return jax.shard_map(fn, mesh=mesh, in_specs=in_specs, out_specs=P(), check_vma=False)
```

```python
import functools

import jax
import jax.numpy as jnp
from jax import lax
from jax.experimental import pallas as pl
from jax.experimental.pallas import tpu as pltpu
from jax.sharding import PartitionSpec as P

DAMPING = 0.1
F32 = jnp.float32
BF16 = jnp.bfloat16


def _shift(x, axis, n, s):
    return lax.ppermute(x, axis, [(i, (i + s) % n) for i in range(n)])


def _place(parts, me, n, dim):
    w = parts[0].shape[dim]
    shape = list(parts[0].shape)
    shape[dim] = n * w
    out = jnp.zeros(shape, parts[0].dtype)
    for s, p in enumerate(parts):
        out = lax.dynamic_update_slice_in_dim(out, p, ((me - s) % n) * w, axis=dim)
    return out


def _gather(x, axis, n, dim):
    me = lax.axis_index(axis)
    return _place([x] + [_shift(x, axis, n, s) for s in range(1, n)], me, n, dim)


def _allreduce_bf16(x, axis, n):
    me = lax.axis_index(axis)
    w = x.shape[1] // n
    total = lax.dynamic_slice_in_dim(x, me * w, w, axis=1)
    for s in range(1, n):
        piece = lax.dynamic_slice_in_dim(x, ((me + s) % n) * w, w, axis=1)
        total = total + _shift(piece, axis, n, s)
    return _gather(total.astype(BF16), axis, n, 1)


def _allreduce_small(x, axis, n):
    stacked = _gather(x[None], axis, n, 0)
    return jnp.sum(stacked, axis=0)


def _lifted_kernel(a_ref, e_ref, q_ref, o_ref):
    recip = 1.0 / (e_ref[...].astype(F32) + DAMPING)
    a = a_ref[...]
    dims = (((1,), (1,)), ((), ()))
    for qi in range(q_ref.shape[0]):
        s = q_ref[qi].astype(F32) * recip
        hi = s.astype(BF16)
        lo = (s - hi.astype(F32)).astype(BF16)
        o_ref[qi] = lax.dot_general(a, hi, dims, preferred_element_type=F32) + lax.dot_general(
            a, lo, dims, preferred_element_type=F32
        )


def _lifted(act_rot, eigenvalues, queries, chunk, nchunks):
    nq, kk, jj = queries.shape
    tt = act_rot.shape[0]
    kc = kk // nchunks
    tk = next(c for c in (512, 256, 128, kc) if kc % c == 0)
    base = chunk * (kc // tk)
    return pl.pallas_call(
        _lifted_kernel,
        grid=(kc // tk,),
        in_specs=[
            pl.BlockSpec((tt, jj), lambda i: (0, 0)),
            pl.BlockSpec((tk, jj), lambda i: (base + i, 0)),
            pl.BlockSpec((nq, tk, jj), lambda i: (0, base + i, 0)),
        ],
        out_specs=pl.BlockSpec((nq, tt, tk), lambda i: (0, 0, i)),
        out_shape=jax.ShapeDtypeStruct((nq, tt, kc), F32),
        compiler_params=pltpu.CompilerParams(dimension_semantics=("arbitrary",)),
        cost_estimate=pl.CostEstimate(
            flops=4 * nq * kc * jj * tt,
            bytes_accessed=(nq + 1) * kc * jj * 2 + nq * tt * kc * 4,
            transcendentals=0,
        ),
    )(act_rot, eigenvalues, queries)


def local(out_grads, in_acts, out_basis, in_basis, eigenvalues, queries, *, nr, nc, ng, nl):
    acts_all = _gather(in_acts, "row", nr, 0)
    grads_all = _gather(out_grads, "col", nc, 0)
    act_part = jnp.dot(acts_all, in_basis, preferred_element_type=F32)
    act_rot = _allreduce_bf16(act_part, "col", nc)
    kk = out_basis.shape[1]
    kg = kk // ng
    grad_part = jnp.concatenate(
        [
            jnp.dot(grads_all, out_basis[:, g * kg : (g + 1) * kg], preferred_element_type=F32)
            for g in range(ng)
        ],
        axis=1,
    )
    grad_rot = _allreduce_bf16(grad_part, "row", nr)
    kc = kk // nl
    partial = None
    for c in range(nl):
        lifted = _lifted(act_rot, eigenvalues, queries, c, nl)
        g = grad_rot[:, c * kc : (c + 1) * kc].astype(F32)
        term = jnp.sum(lifted * g[None], axis=2)
        partial = term if partial is None else partial + term
    return _allreduce_small(_allreduce_small(partial, "col", nc), "row", nr)


def solution(mesh):
    in_specs = (
        P("col", "row"),
        P("row", "col"),
        P("row", "col"),
        P("col", "row"),
        P("col", "row"),
        P(None, "col", "row"),
    )
    fn = functools.partial(local, nr=mesh.shape["row"], nc=mesh.shape["col"], ng=4, nl=4)
    return jax.shard_map(fn, mesh=mesh, in_specs=in_specs, out_specs=P(), check_vma=False)
```

```python
import functools

import jax
import jax.numpy as jnp
from jax import lax
from jax.experimental import pallas as pl
from jax.experimental.pallas import tpu as pltpu
from jax.sharding import PartitionSpec as P

DAMPING = 0.1
F32 = jnp.float32
BF16 = jnp.bfloat16


def _swap(x, axis, n, b):
    return lax.ppermute(x, axis, [(i, i ^ b) for i in range(n)])


def _gather(x, axis, n, dim):
    me = lax.axis_index(axis)
    b = 1
    while b < n:
        other = _swap(x, axis, n, b)
        first = (me // b) % 2 == 0
        x = jnp.where(first, jnp.concatenate([x, other], dim), jnp.concatenate([other, x], dim))
        b *= 2
    return x


def _allreduce_bf16(x, axis, n, dim, works=()):
    me = lax.axis_index(axis)
    works = list(works)
    done = []

    def swap(v, b):
        if not works:
            return _swap(v, axis, n, b)
        work, arg = works.pop(0)
        v, arg = lax.optimization_barrier((v, arg))
        result = work(arg)
        other = _swap(v, axis, n, b)
        other, result = lax.optimization_barrier((other, result))
        done.append(result)
        return other

    b = 1
    while b < n:
        half = x.shape[dim] // 2
        upper = (me // b) % 2 == 1
        lo = lax.slice_in_dim(x, 0, half, axis=dim)
        hi = lax.slice_in_dim(x, half, 2 * half, axis=dim)
        keep = jnp.where(upper, hi, lo)
        send = jnp.where(upper, lo, hi)
        x = keep + swap(send, b)
        b *= 2
    x = x.astype(BF16)
    b = n // 2
    while b >= 1:
        other = swap(x, b)
        first = (me // b) % 2 == 0
        x = jnp.where(first, jnp.concatenate([x, other], dim), jnp.concatenate([other, x], dim))
        b //= 2
    done += [work(arg) for work, arg in works]
    return x, done


def _allreduce_small(x, axis, n):
    b = 1
    while b < n:
        x = x + _swap(x, axis, n, b)
        b *= 2
    return x


def _lifted_kernel(a_ref, e_ref, q_ref, o_ref):
    recip = 1.0 / (e_ref[...].astype(F32) + DAMPING)
    a = a_ref[...]
    dims = (((1,), (1,)), ((), ()))
    for qi in range(q_ref.shape[0]):
        s = q_ref[qi].astype(F32) * recip
        hi = s.astype(BF16)
        lo = (s - hi.astype(F32)).astype(BF16)
        o_ref[qi] = lax.dot_general(a, hi, dims, preferred_element_type=F32) + lax.dot_general(
            a, lo, dims, preferred_element_type=F32
        )


def _lifted(act_rot, eigenvalues, queries, t0, t1, tk):
    nq, kk, jj = queries.shape
    tt = act_rot.shape[0]
    kc = (t1 - t0) * tk
    return pl.pallas_call(
        _lifted_kernel,
        grid=(t1 - t0,),
        in_specs=[
            pl.BlockSpec((tt, jj), lambda i: (0, 0)),
            pl.BlockSpec((tk, jj), lambda i: (t0 + i, 0)),
            pl.BlockSpec((nq, tk, jj), lambda i: (0, t0 + i, 0)),
        ],
        out_specs=pl.BlockSpec((nq, tt, tk), lambda i: (0, 0, i)),
        out_shape=jax.ShapeDtypeStruct((nq, tt, kc), F32),
        compiler_params=pltpu.CompilerParams(
            dimension_semantics=("arbitrary",), vmem_limit_bytes=48 * 1024 * 1024
        ),
        cost_estimate=pl.CostEstimate(
            flops=4 * nq * kc * jj * tt,
            bytes_accessed=(nq + 1) * kc * jj * 2 + nq * tt * kc * 4,
            transcendentals=0,
        ),
    )(act_rot, eigenvalues, queries)


def local(out_grads, in_acts, out_basis, in_basis, eigenvalues, queries, *, nr, nc, nl):
    acts_all = _gather(in_acts, "row", nr, 0)
    grads_all = _gather(out_grads, "col", nc, 0)
    act_part = jnp.dot(acts_all, in_basis, preferred_element_type=F32)
    act_rot, _ = _allreduce_bf16(act_part, "col", nc, 1)
    grads_all, act_rot = lax.optimization_barrier((grads_all, act_rot))
    grad_part = jnp.dot(grads_all, out_basis, preferred_element_type=F32)
    kk = queries.shape[1]
    tk = next(c for c in (512, 256, 128, kk) if kk % c == 0)
    nt = kk // tk
    bounds = [round(i * nt / nl) for i in range(nl + 1)]
    spans = [(t0, t1) for t0, t1 in zip(bounds[:-1], bounds[1:]) if t1 > t0]
    works = [
        (functools.partial(lambda a, t0, t1: _lifted(a, eigenvalues, queries, t0, t1, tk), t0=t0, t1=t1), act_rot)
        for t0, t1 in spans
    ]
    grad_rot, lifted = _allreduce_bf16(grad_part, "row", nr, 1, works)
    partial = None
    for (t0, t1), piece in zip(spans, lifted):
        g = grad_rot[:, t0 * tk : t1 * tk].astype(F32)
        term = jnp.sum(piece * g[None], axis=2)
        partial = term if partial is None else partial + term
    return _allreduce_small(_allreduce_small(partial, "col", nc), "row", nr)


def solution(mesh):
    in_specs = (
        P("col", "row"),
        P("row", "col"),
        P("row", "col"),
        P("col", "row"),
        P("col", "row"),
        P(None, "col", "row"),
    )
    fn = functools.partial(local, nr=mesh.shape["row"], nc=mesh.shape["col"], nl=6)
    return jax.shard_map(fn, mesh=mesh, in_specs=in_specs, out_specs=P(), check_vma=False)
```

```python
import functools

import jax
import jax.numpy as jnp
from jax import lax
from jax.experimental import pallas as pl
from jax.experimental.pallas import tpu as pltpu
from jax.sharding import PartitionSpec as P

DAMPING = 0.1
F32 = jnp.float32
BF16 = jnp.bfloat16


def _swap(x, axis, n, b):
    return lax.ppermute(x, axis, [(i, i ^ b) for i in range(n)])


def _gather(x, axis, n, dim):
    me = lax.axis_index(axis)
    b = 1
    while b < n:
        other = _swap(x, axis, n, b)
        first = (me // b) % 2 == 0
        x = jnp.where(first, jnp.concatenate([x, other], dim), jnp.concatenate([other, x], dim))
        b *= 2
    return x


def _allreduce_bf16(x, axis, n, dim, works=()):
    me = lax.axis_index(axis)
    works = list(works)
    done = []

    def swap(v, b):
        if not works:
            return _swap(v, axis, n, b)
        work, arg = works.pop(0)
        v, arg = lax.optimization_barrier((v, arg))
        result = work(arg)
        other = _swap(v, axis, n, b)
        other, result = lax.optimization_barrier((other, result))
        done.append(result)
        return other

    b = 1
    while b < n:
        half = x.shape[dim] // 2
        upper = (me // b) % 2 == 1
        lo = lax.slice_in_dim(x, 0, half, axis=dim)
        hi = lax.slice_in_dim(x, half, 2 * half, axis=dim)
        keep = jnp.where(upper, hi, lo)
        send = jnp.where(upper, lo, hi)
        x = keep + swap(send, b)
        b *= 2
    x = x.astype(BF16)
    b = n // 2
    while b >= 1:
        other = swap(x, b)
        first = (me // b) % 2 == 0
        x = jnp.where(first, jnp.concatenate([x, other], dim), jnp.concatenate([other, x], dim))
        b //= 2
    done += [work(arg) for work, arg in works]
    return x, done


def _allreduce_small(x, axis, n):
    b = 1
    while b < n:
        x = x + _swap(x, axis, n, b)
        b *= 2
    return x


def _lifted_kernel(a_ref, e_ref, q_ref, o_ref):
    recip = 1.0 / (e_ref[...].astype(F32) + DAMPING)
    a = a_ref[...]
    dims = (((1,), (1,)), ((), ()))
    for qi in range(q_ref.shape[0]):
        s = q_ref[qi].astype(F32) * recip
        hi = s.astype(BF16)
        lo = (s - hi.astype(F32)).astype(BF16)
        o_ref[qi] = lax.dot_general(a, hi, dims, preferred_element_type=F32) + lax.dot_general(
            a, lo, dims, preferred_element_type=F32
        )


def _lifted(act_rot, eigenvalues, queries, t0, t1, tk):
    nq, kk, jj = queries.shape
    tt = act_rot.shape[0]
    kc = (t1 - t0) * tk
    return pl.pallas_call(
        _lifted_kernel,
        grid=(t1 - t0,),
        in_specs=[
            pl.BlockSpec((tt, jj), lambda i: (0, 0)),
            pl.BlockSpec((tk, jj), lambda i: (t0 + i, 0)),
            pl.BlockSpec((nq, tk, jj), lambda i: (0, t0 + i, 0)),
        ],
        out_specs=pl.BlockSpec((nq, tt, tk), lambda i: (0, 0, i)),
        out_shape=jax.ShapeDtypeStruct((nq, tt, kc), F32),
        compiler_params=pltpu.CompilerParams(
            dimension_semantics=("arbitrary",), vmem_limit_bytes=48 * 1024 * 1024
        ),
        cost_estimate=pl.CostEstimate(
            flops=4 * nq * kc * jj * tt,
            bytes_accessed=(nq + 1) * kc * jj * 2 + nq * tt * kc * 4,
            transcendentals=0,
        ),
    )(act_rot, eigenvalues, queries)


def local(out_grads, in_acts, out_basis, in_basis, eigenvalues, queries, *, nr, nc, nl, ng):
    acts_all = _gather(in_acts, "row", nr, 0)
    grads_all = _gather(out_grads, "col", nc, 0)
    act_part = jnp.dot(acts_all, in_basis, preferred_element_type=F32)
    kg = out_basis.shape[1] // ng
    grad_works = [
        (functools.partial(lambda g, c: jnp.dot(g, out_basis[:, c * kg : (c + 1) * kg], preferred_element_type=F32), c=c), grads_all)
        for c in range(ng)
    ]
    act_rot, grad_parts = _allreduce_bf16(act_part, "col", nc, 1, grad_works)
    grad_part = jnp.concatenate(grad_parts, axis=1)
    kk = queries.shape[1]
    tk = next(c for c in (512, 256, 128, kk) if kk % c == 0)
    nt = kk // tk
    bounds = [round(i * nt / nl) for i in range(nl + 1)]
    spans = [(t0, t1) for t0, t1 in zip(bounds[:-1], bounds[1:]) if t1 > t0]
    works = [
        (functools.partial(lambda a, t0, t1: _lifted(a, eigenvalues, queries, t0, t1, tk), t0=t0, t1=t1), act_rot)
        for t0, t1 in spans
    ]
    grad_rot, lifted = _allreduce_bf16(grad_part, "row", nr, 1, works)
    partial = None
    for (t0, t1), piece in zip(spans, lifted):
        g = grad_rot[:, t0 * tk : t1 * tk].astype(F32)
        term = jnp.sum(piece * g[None], axis=2)
        partial = term if partial is None else partial + term
    return _allreduce_small(_allreduce_small(partial, "col", nc), "row", nr)


def solution(mesh):
    in_specs = (
        P("col", "row"),
        P("row", "col"),
        P("row", "col"),
        P("col", "row"),
        P("col", "row"),
        P(None, "col", "row"),
    )
    fn = functools.partial(local, nr=mesh.shape["row"], nc=mesh.shape["col"], nl=6, ng=4)
    return jax.shard_map(fn, mesh=mesh, in_specs=in_specs, out_specs=P(), check_vma=False)
```

```python
import functools

import jax
import jax.numpy as jnp
from jax import lax
from jax.experimental import pallas as pl
from jax.experimental.pallas import tpu as pltpu
from jax.sharding import PartitionSpec as P

DAMPING = 0.1
F32 = jnp.float32
BF16 = jnp.bfloat16


def _swap(x, axis, n, b):
    return lax.ppermute(x, axis, [(i, i ^ b) for i in range(n)])


def _gather(x, axis, n, dim):
    me = lax.axis_index(axis)
    b = 1
    while b < n:
        other = _swap(x, axis, n, b)
        first = (me // b) % 2 == 0
        x = jnp.where(first, jnp.concatenate([x, other], dim), jnp.concatenate([other, x], dim))
        b *= 2
    return x


def _allreduce_bf16(x, axis, n, dim, works=()):
    me = lax.axis_index(axis)
    works = list(works)
    done = []

    def swap(v, b):
        if not works:
            return _swap(v, axis, n, b)
        work, arg = works.pop(0)
        if work is None:
            return _swap(v, axis, n, b)
        v, arg = lax.optimization_barrier((v, arg))
        result = work(arg)
        other = _swap(v, axis, n, b)
        other, result = lax.optimization_barrier((other, result))
        done.append(result)
        return other

    b = 1
    while b < n:
        half = x.shape[dim] // 2
        upper = (me // b) % 2 == 1
        lo = lax.slice_in_dim(x, 0, half, axis=dim)
        hi = lax.slice_in_dim(x, half, 2 * half, axis=dim)
        keep = jnp.where(upper, hi, lo)
        send = jnp.where(upper, lo, hi)
        x = keep + swap(send, b)
        b *= 2
    x = x.astype(BF16)
    b = n // 2
    while b >= 1:
        other = swap(x, b)
        first = (me // b) % 2 == 0
        x = jnp.where(first, jnp.concatenate([x, other], dim), jnp.concatenate([other, x], dim))
        b //= 2
    done += [work(arg) for work, arg in works if work is not None]
    return x, done


def _allreduce_small(x, axis, n):
    b = 1
    while b < n:
        x = x + _swap(x, axis, n, b)
        b *= 2
    return x


def _lifted_kernel(a_ref, e_ref, q_ref, o_ref):
    recip = 1.0 / (e_ref[...].astype(F32) + DAMPING)
    a = a_ref[...]
    dims = (((1,), (1,)), ((), ()))
    for qi in range(q_ref.shape[0]):
        s = q_ref[qi].astype(F32) * recip
        hi = s.astype(BF16)
        lo = (s - hi.astype(F32)).astype(BF16)
        o_ref[qi] = lax.dot_general(a, hi, dims, preferred_element_type=F32) + lax.dot_general(
            a, lo, dims, preferred_element_type=F32
        )


def _lifted(act_rot, eigenvalues, queries, t0, t1, tk):
    nq, kk, jj = queries.shape
    tt = act_rot.shape[0]
    kc = (t1 - t0) * tk
    return pl.pallas_call(
        _lifted_kernel,
        grid=(t1 - t0,),
        in_specs=[
            pl.BlockSpec((tt, jj), lambda i: (0, 0)),
            pl.BlockSpec((tk, jj), lambda i: (t0 + i, 0)),
            pl.BlockSpec((nq, tk, jj), lambda i: (0, t0 + i, 0)),
        ],
        out_specs=pl.BlockSpec((nq, tt, tk), lambda i: (0, 0, i)),
        out_shape=jax.ShapeDtypeStruct((nq, tt, kc), F32),
        compiler_params=pltpu.CompilerParams(
            dimension_semantics=("arbitrary",), vmem_limit_bytes=48 * 1024 * 1024
        ),
        cost_estimate=pl.CostEstimate(
            flops=4 * nq * kc * jj * tt,
            bytes_accessed=(nq + 1) * kc * jj * 2 + nq * tt * kc * 4,
            transcendentals=0,
        ),
    )(act_rot, eigenvalues, queries)


def local(out_grads, in_acts, out_basis, in_basis, eigenvalues, queries, *, nr, nc, nl, ng):
    acts_all = _gather(in_acts, "row", nr, 0)
    grads_all = _gather(out_grads, "col", nc, 0)
    act_part = jnp.dot(acts_all, in_basis, preferred_element_type=F32)
    nb = out_basis.shape[1] // 128
    cuts = [128 * round(i * nb / ng) for i in range(ng + 1)]
    grad_works = [(None, None)] + [
        (functools.partial(lambda g, c0, c1: jnp.dot(g, out_basis[:, c0:c1], preferred_element_type=F32), c0=c0, c1=c1), grads_all)
        for c0, c1 in zip(cuts[:-1], cuts[1:])
    ]
    act_rot, grad_parts = _allreduce_bf16(act_part, "col", nc, 1, grad_works)
    grad_part = jnp.concatenate(grad_parts, axis=1)
    kk = queries.shape[1]
    tk = next(c for c in (512, 256, 128, kk) if kk % c == 0)
    nt = kk // tk
    bounds = [round(i * nt / nl) for i in range(nl + 1)]
    spans = [(t0, t1) for t0, t1 in zip(bounds[:-1], bounds[1:]) if t1 > t0]
    works = [
        (functools.partial(lambda a, t0, t1: _lifted(a, eigenvalues, queries, t0, t1, tk), t0=t0, t1=t1), act_rot)
        for t0, t1 in spans
    ]
    grad_rot, lifted = _allreduce_bf16(grad_part, "row", nr, 1, works)
    partial = None
    for (t0, t1), piece in zip(spans, lifted):
        g = grad_rot[:, t0 * tk : t1 * tk].astype(F32)
        term = jnp.sum(piece * g[None], axis=2)
        partial = term if partial is None else partial + term
    return _allreduce_small(_allreduce_small(partial, "col", nc), "row", nr)


def solution(mesh):
    in_specs = (
        P("col", "row"),
        P("row", "col"),
        P("row", "col"),
        P("col", "row"),
        P("col", "row"),
        P(None, "col", "row"),
    )
    fn = functools.partial(local, nr=mesh.shape["row"], nc=mesh.shape["col"], nl=6, ng=3)
    return jax.shard_map(fn, mesh=mesh, in_specs=in_specs, out_specs=P(), check_vma=False)
```

```python
import functools

import jax
import jax.numpy as jnp
from jax import lax
from jax.experimental import pallas as pl
from jax.experimental.pallas import tpu as pltpu
from jax.sharding import PartitionSpec as P

DAMPING = 0.1
F32 = jnp.float32
BF16 = jnp.bfloat16


def _swap(x, axis, n, b):
    return lax.ppermute(x, axis, [(i, i ^ b) for i in range(n)])


def _gather(x, axis, n, dim):
    me = lax.axis_index(axis)
    b = 1
    while b < n:
        other = _swap(x, axis, n, b)
        first = (me // b) % 2 == 0
        x = jnp.where(first, jnp.concatenate([x, other], dim), jnp.concatenate([other, x], dim))
        b *= 2
    return x


def _gather_far_first(x, axis, n):
    me = lax.axis_index(axis)
    y = x[None]
    b = n // 2
    while b >= 1:
        other = _swap(y, axis, n, b)
        first = (me // b) % 2 == 0
        lo = jnp.where(first, y, other)
        hi = jnp.where(first, other, y)
        y = jnp.stack([lo, hi], axis=1).reshape((2 * y.shape[0],) + x.shape)
        b //= 2
    return y.reshape((n * x.shape[0],) + x.shape[1:])


def _allreduce_bf16(x, axis, n, dim, works=()):
    me = lax.axis_index(axis)
    works = list(works)
    done = []

    def swap(v, b):
        if not works:
            return _swap(v, axis, n, b)
        work, arg = works.pop(0)
        if work is None:
            return _swap(v, axis, n, b)
        v, arg = lax.optimization_barrier((v, arg))
        result = work(arg)
        other = _swap(v, axis, n, b)
        other, result = lax.optimization_barrier((other, result))
        done.append(result)
        return other

    b = 1
    while b < n:
        half = x.shape[dim] // 2
        upper = (me // b) % 2 == 1
        lo = lax.slice_in_dim(x, 0, half, axis=dim)
        hi = lax.slice_in_dim(x, half, 2 * half, axis=dim)
        keep = jnp.where(upper, hi, lo)
        send = jnp.where(upper, lo, hi)
        x = keep + swap(send, b)
        b *= 2
    x = x.astype(BF16)
    b = n // 2
    while b >= 1:
        other = swap(x, b)
        first = (me // b) % 2 == 0
        x = jnp.where(first, jnp.concatenate([x, other], dim), jnp.concatenate([other, x], dim))
        b //= 2
    done += [work(arg) for work, arg in works if work is not None]
    return x, done


def _allreduce_small(x, axis, n):
    b = 1
    while b < n:
        x = x + _swap(x, axis, n, b)
        b *= 2
    return x


def _lifted_kernel(a_ref, e_ref, q_ref, o_ref):
    recip = 1.0 / (e_ref[...].astype(F32) + DAMPING)
    a = a_ref[...]
    dims = (((1,), (1,)), ((), ()))
    for qi in range(q_ref.shape[0]):
        s = q_ref[qi].astype(F32) * recip
        hi = s.astype(BF16)
        lo = (s - hi.astype(F32)).astype(BF16)
        o_ref[qi] = lax.dot_general(a, hi, dims, preferred_element_type=F32) + lax.dot_general(
            a, lo, dims, preferred_element_type=F32
        )


def _lifted(act_rot, eigenvalues, queries, t0, t1, tk):
    nq, kk, jj = queries.shape
    tt = act_rot.shape[0]
    kc = (t1 - t0) * tk
    return pl.pallas_call(
        _lifted_kernel,
        grid=(t1 - t0,),
        in_specs=[
            pl.BlockSpec((tt, jj), lambda i: (0, 0)),
            pl.BlockSpec((tk, jj), lambda i: (t0 + i, 0)),
            pl.BlockSpec((nq, tk, jj), lambda i: (0, t0 + i, 0)),
        ],
        out_specs=pl.BlockSpec((nq, tt, tk), lambda i: (0, 0, i)),
        out_shape=jax.ShapeDtypeStruct((nq, tt, kc), F32),
        compiler_params=pltpu.CompilerParams(
            dimension_semantics=("arbitrary",), vmem_limit_bytes=48 * 1024 * 1024
        ),
        cost_estimate=pl.CostEstimate(
            flops=4 * nq * kc * jj * tt,
            bytes_accessed=(nq + 1) * kc * jj * 2 + nq * tt * kc * 4,
            transcendentals=0,
        ),
    )(act_rot, eigenvalues, queries)


def local(out_grads, in_acts, out_basis, in_basis, eigenvalues, queries, *, nr, nc, nl, ng):
    acts_all = _gather(in_acts, "row", nr, 0)
    grads_all = _gather_far_first(out_grads, "col", nc)
    act_part = jnp.dot(acts_all, in_basis, preferred_element_type=F32)
    nb = out_basis.shape[1] // 128
    cuts = [128 * round(i * nb / ng) for i in range(ng + 1)]
    grad_works = [(None, None)] + [
        (functools.partial(lambda g, c0, c1: jnp.dot(g, out_basis[:, c0:c1], preferred_element_type=F32), c0=c0, c1=c1), grads_all)
        for c0, c1 in zip(cuts[:-1], cuts[1:])
    ]
    act_rot, grad_parts = _allreduce_bf16(act_part, "col", nc, 1, grad_works)
    grad_part = jnp.concatenate(grad_parts, axis=1)
    kk = queries.shape[1]
    tk = next(c for c in (512, 256, 128, kk) if kk % c == 0)
    nt = kk // tk
    weights = [2, 4, 2, 2, 2, 2] if nl == 6 else [1] * nl
    acc = [0]
    for w in weights:
        acc.append(acc[-1] + w)
    bounds = [round(a * nt / acc[-1]) for a in acc]
    spans = [(t0, t1) for t0, t1 in zip(bounds[:-1], bounds[1:]) if t1 > t0]
    works = [
        (functools.partial(lambda a, t0, t1: _lifted(a, eigenvalues, queries, t0, t1, tk), t0=t0, t1=t1), act_rot)
        for t0, t1 in spans
    ]
    grad_rot, lifted = _allreduce_bf16(grad_part, "row", nr, 1, works)
    partial = None
    for (t0, t1), piece in zip(spans, lifted):
        g = grad_rot[:, t0 * tk : t1 * tk].astype(F32)
        term = jnp.sum(piece * g[None], axis=2)
        partial = term if partial is None else partial + term
    return _allreduce_small(_allreduce_small(partial, "col", nc), "row", nr)


def solution(mesh):
    in_specs = (
        P("col", "row"),
        P("row", "col"),
        P("row", "col"),
        P("col", "row"),
        P("col", "row"),
        P(None, "col", "row"),
    )
    fn = functools.partial(local, nr=mesh.shape["row"], nc=mesh.shape["col"], nl=6, ng=3)
    return jax.shard_map(fn, mesh=mesh, in_specs=in_specs, out_specs=P(), check_vma=False)
```

```python
import functools

import jax
import jax.numpy as jnp
from jax import lax
from jax.experimental import pallas as pl
from jax.experimental.pallas import tpu as pltpu
from jax.sharding import PartitionSpec as P

DAMPING = 0.1
F32 = jnp.float32
BF16 = jnp.bfloat16


def _swap(x, axis, n, b):
    return lax.ppermute(x, axis, [(i, i ^ b) for i in range(n)])


def _gather(x, axis, n, dim):
    me = lax.axis_index(axis)
    b = 1
    while b < n:
        other = _swap(x, axis, n, b)
        first = (me // b) % 2 == 0
        x = jnp.where(first, jnp.concatenate([x, other], dim), jnp.concatenate([other, x], dim))
        b *= 2
    return x


def _gather_far_first(x, axis, n):
    me = lax.axis_index(axis)
    y = x[None]
    b = n // 2
    while b >= 1:
        other = _swap(y, axis, n, b)
        first = (me // b) % 2 == 0
        lo = jnp.where(first, y, other)
        hi = jnp.where(first, other, y)
        y = jnp.stack([lo, hi], axis=1).reshape((2 * y.shape[0],) + x.shape)
        b //= 2
    return y.reshape((n * x.shape[0],) + x.shape[1:])


def _allreduce_bf16(x, axis, n, dim, works=()):
    me = lax.axis_index(axis)
    works = list(works)
    done = []

    def swap(v, b):
        if not works:
            return _swap(v, axis, n, b)
        work, arg = works.pop(0)
        if work is None:
            return _swap(v, axis, n, b)
        v, arg = lax.optimization_barrier((v, arg))
        result = work(arg)
        other = _swap(v, axis, n, b)
        other, result = lax.optimization_barrier((other, result))
        done.append(result)
        return other

    b = 1
    while b < n:
        half = x.shape[dim] // 2
        upper = (me // b) % 2 == 1
        lo = lax.slice_in_dim(x, 0, half, axis=dim)
        hi = lax.slice_in_dim(x, half, 2 * half, axis=dim)
        keep = jnp.where(upper, hi, lo)
        send = jnp.where(upper, lo, hi)
        x = keep + swap(send, b)
        b *= 2
    x = x.astype(BF16)
    b = n // 2
    while b >= 1:
        other = swap(x, b)
        first = (me // b) % 2 == 0
        x = jnp.where(first, jnp.concatenate([x, other], dim), jnp.concatenate([other, x], dim))
        b //= 2
    done += [work(arg) for work, arg in works if work is not None]
    return x, done


def _allreduce_small(x, axis, n):
    b = 1
    while b < n:
        x = x + _swap(x, axis, n, b)
        b *= 2
    return x


def _lifted_kernel(a_ref, e_ref, q_ref, o_ref):
    recip = 1.0 / (e_ref[...].astype(F32) + DAMPING)
    a = a_ref[...]
    dims = (((1,), (1,)), ((), ()))
    for qi in range(q_ref.shape[0]):
        s = (q_ref[qi].astype(F32) * recip).astype(BF16)
        o_ref[qi] = lax.dot_general(a, s, dims, preferred_element_type=F32)


def _lifted(act_rot, eigenvalues, queries, t0, t1, tk):
    nq, kk, jj = queries.shape
    tt = act_rot.shape[0]
    kc = (t1 - t0) * tk
    return pl.pallas_call(
        _lifted_kernel,
        grid=(t1 - t0,),
        in_specs=[
            pl.BlockSpec((tt, jj), lambda i: (0, 0)),
            pl.BlockSpec((tk, jj), lambda i: (t0 + i, 0)),
            pl.BlockSpec((nq, tk, jj), lambda i: (0, t0 + i, 0)),
        ],
        out_specs=pl.BlockSpec((nq, tt, tk), lambda i: (0, 0, i)),
        out_shape=jax.ShapeDtypeStruct((nq, tt, kc), F32),
        compiler_params=pltpu.CompilerParams(
            dimension_semantics=("arbitrary",), vmem_limit_bytes=48 * 1024 * 1024
        ),
        cost_estimate=pl.CostEstimate(
            flops=2 * nq * kc * jj * tt,
            bytes_accessed=(nq + 1) * kc * jj * 2 + nq * tt * kc * 4,
            transcendentals=0,
        ),
    )(act_rot, eigenvalues, queries)


def local(out_grads, in_acts, out_basis, in_basis, eigenvalues, queries, *, nr, nc, nl, ng):
    acts_all = _gather(in_acts, "row", nr, 0)
    grads_all = _gather_far_first(out_grads, "col", nc)
    act_part = jnp.dot(acts_all, in_basis, preferred_element_type=F32)
    nb = out_basis.shape[1] // 128
    cuts = [128 * round(i * nb / ng) for i in range(ng + 1)]
    grad_works = [(None, None)] + [
        (functools.partial(lambda g, c0, c1: jnp.dot(g, out_basis[:, c0:c1], preferred_element_type=F32), c0=c0, c1=c1), grads_all)
        for c0, c1 in zip(cuts[:-1], cuts[1:])
    ]
    act_rot, grad_parts = _allreduce_bf16(act_part, "col", nc, 1, grad_works)
    grad_part = jnp.concatenate(grad_parts, axis=1)
    kk = queries.shape[1]
    tk = next(c for c in (512, 256, 128, kk) if kk % c == 0)
    nt = kk // tk
    weights = [2, 5, 2, 2, 2, 1] if nl == 6 else [1] * nl
    acc = [0]
    for w in weights:
        acc.append(acc[-1] + w)
    bounds = [round(a * nt / acc[-1]) for a in acc]
    spans = [(t0, t1) for t0, t1 in zip(bounds[:-1], bounds[1:]) if t1 > t0]
    works = [
        (functools.partial(lambda a, t0, t1: _lifted(a, eigenvalues, queries, t0, t1, tk), t0=t0, t1=t1), act_rot)
        for t0, t1 in spans
    ]
    grad_rot, lifted = _allreduce_bf16(grad_part, "row", nr, 1, works)
    partial = None
    for (t0, t1), piece in zip(spans, lifted):
        g = grad_rot[:, t0 * tk : t1 * tk].astype(F32)
        term = jnp.sum(piece * g[None], axis=2)
        partial = term if partial is None else partial + term
    return _allreduce_small(_allreduce_small(partial, "col", nc), "row", nr)


def solution(mesh):
    in_specs = (
        P("col", "row"),
        P("row", "col"),
        P("row", "col"),
        P("col", "row"),
        P("col", "row"),
        P(None, "col", "row"),
    )
    fn = functools.partial(local, nr=mesh.shape["row"], nc=mesh.shape["col"], nl=6, ng=3)
    return jax.shard_map(fn, mesh=mesh, in_specs=in_specs, out_specs=P(), check_vma=False)
```

```python
import functools

import jax
import jax.numpy as jnp
from jax import lax
from jax.experimental import pallas as pl
from jax.experimental.pallas import tpu as pltpu
from jax.sharding import PartitionSpec as P

DAMPING = 0.1
F32 = jnp.float32
BF16 = jnp.bfloat16


def _swap(x, axis, n, b):
    return lax.ppermute(x, axis, [(i, i ^ b) for i in range(n)])


def _gather(x, axis, n, dim):
    me = lax.axis_index(axis)
    b = 1
    while b < n:
        other = _swap(x, axis, n, b)
        first = (me // b) % 2 == 0
        x = jnp.where(first, jnp.concatenate([x, other], dim), jnp.concatenate([other, x], dim))
        b *= 2
    return x


def _gather_far_first(x, axis, n):
    me = lax.axis_index(axis)
    y = x[None]
    b = n // 2
    while b >= 1:
        other = _swap(y, axis, n, b)
        first = (me // b) % 2 == 0
        lo = jnp.where(first, y, other)
        hi = jnp.where(first, other, y)
        y = jnp.stack([lo, hi], axis=1).reshape((2 * y.shape[0],) + x.shape)
        b //= 2
    return y.reshape((n * x.shape[0],) + x.shape[1:])


def _allreduce_bf16(x, axis, n, dim, works=(), paths=1):
    me = lax.axis_index(axis)
    bits = []
    b = 1
    while b < n:
        bits.append(b)
        b *= 2
    orders = [bits, bits[:1] + bits[:0:-1]][:paths]
    works = list(works)
    done = []

    def swap(vs, bs):
        work, arg = works.pop(0) if works else (None, None)
        if work is None:
            return [_swap(v, axis, n, b) for v, b in zip(vs, bs)]
        *vs, arg = lax.optimization_barrier((*vs, arg))
        result = work(arg)
        others = [_swap(v, axis, n, b) for v, b in zip(vs, bs)]
        *others, result = lax.optimization_barrier((*others, result))
        done.append(result)
        return others

    w = x.shape[dim] // len(orders)
    xs = [lax.slice_in_dim(x, p * w, (p + 1) * w, axis=dim) for p in range(len(orders))]
    for r in range(len(bits)):
        keeps, sends = [], []
        for p, v in enumerate(xs):
            b = orders[p][r]
            half = v.shape[dim] // 2
            upper = (me // b) % 2 == 1
            lo = lax.slice_in_dim(v, 0, half, axis=dim)
            hi = lax.slice_in_dim(v, half, 2 * half, axis=dim)
            keeps.append(jnp.where(upper, hi, lo))
            sends.append(jnp.where(upper, lo, hi))
        others = swap(sends, [o[r] for o in orders])
        xs = [k + o for k, o in zip(keeps, others)]
    xs = [v.astype(BF16) for v in xs]
    for r in reversed(range(len(bits))):
        others = swap(xs, [o[r] for o in orders])
        new = []
        for p, (v, other) in enumerate(zip(xs, others)):
            first = (me // orders[p][r]) % 2 == 0
            new.append(jnp.where(first, jnp.concatenate([v, other], dim), jnp.concatenate([other, v], dim)))
        xs = new
    done += [work(arg) for work, arg in works if work is not None]
    return jnp.concatenate(xs, dim) if len(xs) > 1 else xs[0], done


def _allreduce_small(x, axis, n):
    b = 1
    while b < n:
        x = x + _swap(x, axis, n, b)
        b *= 2
    return x


def _lifted_kernel(a_ref, e_ref, q_ref, o_ref):
    recip = 1.0 / (e_ref[...].astype(F32) + DAMPING)
    a = a_ref[...]
    dims = (((1,), (1,)), ((), ()))
    for qi in range(q_ref.shape[0]):
        s = (q_ref[qi].astype(F32) * recip).astype(BF16)
        o_ref[qi] = lax.dot_general(a, s, dims, preferred_element_type=F32)


def _lifted(act_rot, eigenvalues, queries, t0, t1, tk):
    nq, kk, jj = queries.shape
    tt = act_rot.shape[0]
    kc = (t1 - t0) * tk
    return pl.pallas_call(
        _lifted_kernel,
        grid=(t1 - t0,),
        in_specs=[
            pl.BlockSpec((tt, jj), lambda i: (0, 0)),
            pl.BlockSpec((tk, jj), lambda i: (t0 + i, 0)),
            pl.BlockSpec((nq, tk, jj), lambda i: (0, t0 + i, 0)),
        ],
        out_specs=pl.BlockSpec((nq, tt, tk), lambda i: (0, 0, i)),
        out_shape=jax.ShapeDtypeStruct((nq, tt, kc), F32),
        compiler_params=pltpu.CompilerParams(
            dimension_semantics=("arbitrary",), vmem_limit_bytes=48 * 1024 * 1024
        ),
        cost_estimate=pl.CostEstimate(
            flops=2 * nq * kc * jj * tt,
            bytes_accessed=(nq + 1) * kc * jj * 2 + nq * tt * kc * 4,
            transcendentals=0,
        ),
    )(act_rot, eigenvalues, queries)


def local(out_grads, in_acts, out_basis, in_basis, eigenvalues, queries, *, nr, nc, nl, ng):
    acts_all = _gather(in_acts, "row", nr, 0)
    grads_all = _gather_far_first(out_grads, "col", nc)
    act_part = jnp.dot(acts_all, in_basis, preferred_element_type=F32)
    nb = out_basis.shape[1] // 128
    cuts = [128 * round(i * nb / ng) for i in range(ng + 1)]
    grad_works = [(None, None)] + [
        (functools.partial(lambda g, c0, c1: jnp.dot(g, out_basis[:, c0:c1], preferred_element_type=F32), c0=c0, c1=c1), grads_all)
        for c0, c1 in zip(cuts[:-1], cuts[1:])
    ]
    act_rot, grad_parts = _allreduce_bf16(act_part, "col", nc, 1, grad_works)
    grad_part = jnp.concatenate(grad_parts, axis=1)
    kk = queries.shape[1]
    tk = next(c for c in (512, 256, 128, kk) if kk % c == 0)
    nt = kk // tk
    weights = [2, 5, 2, 2, 2, 1] if nl == 6 else [1] * nl
    acc = [0]
    for w in weights:
        acc.append(acc[-1] + w)
    bounds = [round(a * nt / acc[-1]) for a in acc]
    spans = [(t0, t1) for t0, t1 in zip(bounds[:-1], bounds[1:]) if t1 > t0]
    works = [
        (functools.partial(lambda a, t0, t1: _lifted(a, eigenvalues, queries, t0, t1, tk), t0=t0, t1=t1), act_rot)
        for t0, t1 in spans
    ]
    grad_rot, lifted = _allreduce_bf16(grad_part, "row", nr, 1, works, paths=2)
    partial = None
    for (t0, t1), piece in zip(spans, lifted):
        g = grad_rot[:, t0 * tk : t1 * tk].astype(F32)
        term = jnp.sum(piece * g[None], axis=2)
        partial = term if partial is None else partial + term
    return _allreduce_small(_allreduce_small(partial, "col", nc), "row", nr)


def solution(mesh):
    in_specs = (
        P("col", "row"),
        P("row", "col"),
        P("row", "col"),
        P("col", "row"),
        P("col", "row"),
        P(None, "col", "row"),
    )
    fn = functools.partial(local, nr=mesh.shape["row"], nc=mesh.shape["col"], nl=6, ng=3)
    return jax.shard_map(fn, mesh=mesh, in_specs=in_specs, out_specs=P(), check_vma=False)
```

```python
import functools

import jax
import jax.numpy as jnp
from jax import lax
from jax.experimental import pallas as pl
from jax.experimental.pallas import tpu as pltpu
from jax.sharding import PartitionSpec as P

DAMPING = 0.1
F32 = jnp.float32
BF16 = jnp.bfloat16


def _swap(x, axis, n, b):
    return lax.ppermute(x, axis, [(i, i ^ b) for i in range(n)])


def _gather(x, axis, n, dim):
    me = lax.axis_index(axis)
    b = 1
    while b < n:
        other = _swap(x, axis, n, b)
        first = (me // b) % 2 == 0
        x = jnp.where(first, jnp.concatenate([x, other], dim), jnp.concatenate([other, x], dim))
        b *= 2
    return x


def _gather_far_first(x, axis, n):
    me = lax.axis_index(axis)
    y = x[None]
    b = n // 2
    while b >= 1:
        other = _swap(y, axis, n, b)
        first = (me // b) % 2 == 0
        lo = jnp.where(first, y, other)
        hi = jnp.where(first, other, y)
        y = jnp.stack([lo, hi], axis=1).reshape((2 * y.shape[0],) + x.shape)
        b //= 2
    return y.reshape((n * x.shape[0],) + x.shape[1:])


def _allreduce_bf16(x, axis, n, dim, works=(), paths=1):
    me = lax.axis_index(axis)
    bits = []
    b = 1
    while b < n:
        bits.append(b)
        b *= 2
    orders = [bits, bits[:1] + bits[:0:-1]][:paths]
    works = list(works)
    done = []

    def swap(vs, bs):
        work, arg, *free = works.pop(0) if works else (None, None)
        if work is None:
            return [_swap(v, axis, n, b) for v, b in zip(vs, bs)]
        if not free:
            *vs, arg = lax.optimization_barrier((*vs, arg))
        result = work(arg)
        others = [_swap(v, axis, n, b) for v, b in zip(vs, bs)]
        *others, result = lax.optimization_barrier((*others, result))
        done.append(result)
        return others

    w = x.shape[dim] // len(orders)
    xs = [lax.slice_in_dim(x, p * w, (p + 1) * w, axis=dim) for p in range(len(orders))]
    for r in range(len(bits)):
        keeps, sends = [], []
        for p, v in enumerate(xs):
            b = orders[p][r]
            half = v.shape[dim] // 2
            upper = (me // b) % 2 == 1
            lo = lax.slice_in_dim(v, 0, half, axis=dim)
            hi = lax.slice_in_dim(v, half, 2 * half, axis=dim)
            keeps.append(jnp.where(upper, hi, lo))
            sends.append(jnp.where(upper, lo, hi))
        others = swap(sends, [o[r] for o in orders])
        xs = [k + o for k, o in zip(keeps, others)]
    xs = [v.astype(BF16) for v in xs]
    for r in reversed(range(len(bits))):
        others = swap(xs, [o[r] for o in orders])
        new = []
        for p, (v, other) in enumerate(zip(xs, others)):
            first = (me // orders[p][r]) % 2 == 0
            new.append(jnp.where(first, jnp.concatenate([v, other], dim), jnp.concatenate([other, v], dim)))
        xs = new
    done += [w[0](w[1]) for w in works if w[0] is not None]
    return jnp.concatenate(xs, dim) if len(xs) > 1 else xs[0], done


def _allreduce_small(x, axis, n):
    b = 1
    while b < n:
        x = x + _swap(x, axis, n, b)
        b *= 2
    return x


def _lifted_kernel(a_ref, e_ref, q_ref, o_ref):
    recip = 1.0 / (e_ref[...].astype(F32) + DAMPING)
    a = a_ref[...]
    dims = (((1,), (1,)), ((), ()))
    for qi in range(q_ref.shape[0]):
        s = (q_ref[qi].astype(F32) * recip).astype(BF16)
        o_ref[qi] = lax.dot_general(a, s, dims, preferred_element_type=F32)


def _lifted(act_rot, eigenvalues, queries, t0, t1, tk):
    nq, kk, jj = queries.shape
    tt = act_rot.shape[0]
    kc = (t1 - t0) * tk
    return pl.pallas_call(
        _lifted_kernel,
        grid=(t1 - t0,),
        in_specs=[
            pl.BlockSpec((tt, jj), lambda i: (0, 0)),
            pl.BlockSpec((tk, jj), lambda i: (t0 + i, 0)),
            pl.BlockSpec((nq, tk, jj), lambda i: (0, t0 + i, 0)),
        ],
        out_specs=pl.BlockSpec((nq, tt, tk), lambda i: (0, 0, i)),
        out_shape=jax.ShapeDtypeStruct((nq, tt, kc), F32),
        compiler_params=pltpu.CompilerParams(
            dimension_semantics=("arbitrary",), vmem_limit_bytes=48 * 1024 * 1024
        ),
        cost_estimate=pl.CostEstimate(
            flops=2 * nq * kc * jj * tt,
            bytes_accessed=(nq + 1) * kc * jj * 2 + nq * tt * kc * 4,
            transcendentals=0,
        ),
    )(act_rot, eigenvalues, queries)


def local(out_grads, in_acts, out_basis, in_basis, eigenvalues, queries, *, nr, nc, nl, ng):
    acts_all = _gather(in_acts, "row", nr, 0)
    grads_all = _gather_far_first(out_grads, "col", nc)
    act_part = jnp.dot(acts_all, in_basis, preferred_element_type=F32)
    nb = out_basis.shape[1] // 128
    cuts = [128 * round(i * nb / ng) for i in range(ng + 1)]
    grad_works = [
        (functools.partial(lambda g, c0, c1: jnp.dot(g, out_basis[:, c0:c1], preferred_element_type=F32), c0=c0, c1=c1), grads_all)
        for c0, c1 in zip(cuts[:-1], cuts[1:])
    ]
    grad_works[0] = grad_works[0] + (True,)
    act_rot, grad_parts = _allreduce_bf16(act_part, "col", nc, 1, grad_works)
    grad_part = jnp.concatenate(grad_parts, axis=1)
    kk = queries.shape[1]
    tk = next(c for c in (512, 256, 128, kk) if kk % c == 0)
    nt = kk // tk
    weights = [2, 5, 2, 2, 2, 1] if nl == 6 else [1] * nl
    acc = [0]
    for w in weights:
        acc.append(acc[-1] + w)
    bounds = [round(a * nt / acc[-1]) for a in acc]
    spans = [(t0, t1) for t0, t1 in zip(bounds[:-1], bounds[1:]) if t1 > t0]
    works = [
        (functools.partial(lambda a, t0, t1: _lifted(a, eigenvalues, queries, t0, t1, tk), t0=t0, t1=t1), act_rot)
        for t0, t1 in spans
    ]
    grad_rot, lifted = _allreduce_bf16(grad_part, "row", nr, 1, works, paths=2)
    partial = None
    for (t0, t1), piece in zip(spans, lifted):
        g = grad_rot[:, t0 * tk : t1 * tk].astype(F32)
        term = jnp.sum(piece * g[None], axis=2)
        partial = term if partial is None else partial + term
    return _allreduce_small(_allreduce_small(partial, "col", nc), "row", nr)


def solution(mesh):
    in_specs = (
        P("col", "row"),
        P("row", "col"),
        P("row", "col"),
        P("col", "row"),
        P("col", "row"),
        P(None, "col", "row"),
    )
    fn = functools.partial(local, nr=mesh.shape["row"], nc=mesh.shape["col"], nl=6, ng=4)
    return jax.shard_map(fn, mesh=mesh, in_specs=in_specs, out_specs=P(), check_vma=False)
```

```python
import functools

import jax
import jax.numpy as jnp
from jax import lax
from jax.experimental import pallas as pl
from jax.experimental.pallas import tpu as pltpu
from jax.sharding import PartitionSpec as P

DAMPING = 0.1
F32 = jnp.float32
BF16 = jnp.bfloat16


def _swap(x, axis, n, b):
    return lax.ppermute(x, axis, [(i, i ^ b) for i in range(n)])


def _gather(x, axis, n, dim):
    me = lax.axis_index(axis)
    b = 1
    while b < n:
        other = _swap(x, axis, n, b)
        first = (me // b) % 2 == 0
        x = jnp.where(first, jnp.concatenate([x, other], dim), jnp.concatenate([other, x], dim))
        b *= 2
    return x


def _gather_far_first(x, axis, n):
    me = lax.axis_index(axis)
    y = x[None]
    b = n // 2
    while b >= 1:
        other = _swap(y, axis, n, b)
        first = (me // b) % 2 == 0
        lo = jnp.where(first, y, other)
        hi = jnp.where(first, other, y)
        y = jnp.stack([lo, hi], axis=1).reshape((2 * y.shape[0],) + x.shape)
        b //= 2
    return y.reshape((n * x.shape[0],) + x.shape[1:])


def _allreduce_bf16(x, axis, n, dim, works=(), paths=1):
    me = lax.axis_index(axis)
    bits = []
    b = 1
    while b < n:
        bits.append(b)
        b *= 2
    orders = [bits, bits[:1] + bits[:0:-1]][: max(paths, 1)]
    works = list(works)
    done = []

    def swap(vs, bs):
        work, arg, *free = works.pop(0) if works else (None, None)
        if work is None:
            return [_swap(v, axis, n, b) for v, b in zip(vs, bs)]
        if not free:
            *vs, arg = lax.optimization_barrier((*vs, arg))
        result = work(arg)
        others = [_swap(v, axis, n, b) for v, b in zip(vs, bs)]
        *others, result = lax.optimization_barrier((*others, result))
        done.append(result)
        return others

    if paths == 0:
        for b in bits:
            x = x + swap([x], [b])[0]
        done += [w[0](w[1]) for w in works if w[0] is not None]
        return x.astype(BF16), done
    w = x.shape[dim] // len(orders)
    xs = [lax.slice_in_dim(x, p * w, (p + 1) * w, axis=dim) for p in range(len(orders))]
    for r in range(len(bits)):
        keeps, sends = [], []
        for p, v in enumerate(xs):
            b = orders[p][r]
            half = v.shape[dim] // 2
            upper = (me // b) % 2 == 1
            lo = lax.slice_in_dim(v, 0, half, axis=dim)
            hi = lax.slice_in_dim(v, half, 2 * half, axis=dim)
            keeps.append(jnp.where(upper, hi, lo))
            sends.append(jnp.where(upper, lo, hi))
        others = swap(sends, [o[r] for o in orders])
        xs = [k + o for k, o in zip(keeps, others)]
    xs = [v.astype(BF16) for v in xs]
    for r in reversed(range(len(bits))):
        others = swap(xs, [o[r] for o in orders])
        new = []
        for p, (v, other) in enumerate(zip(xs, others)):
            first = (me // orders[p][r]) % 2 == 0
            new.append(jnp.where(first, jnp.concatenate([v, other], dim), jnp.concatenate([other, v], dim)))
        xs = new
    done += [w[0](w[1]) for w in works if w[0] is not None]
    return jnp.concatenate(xs, dim) if len(xs) > 1 else xs[0], done


def _allreduce_small(x, axis, n):
    b = 1
    while b < n:
        x = x + _swap(x, axis, n, b)
        b *= 2
    return x


def _lifted_kernel(a_ref, e_ref, q_ref, o_ref):
    recip = 1.0 / (e_ref[...].astype(F32) + DAMPING)
    a = a_ref[...]
    dims = (((1,), (1,)), ((), ()))
    for qi in range(q_ref.shape[0]):
        s = (q_ref[qi].astype(F32) * recip).astype(BF16)
        o_ref[qi] = lax.dot_general(a, s, dims, preferred_element_type=F32)


def _lifted(act_rot, eigenvalues, queries, t0, t1, tk):
    nq, kk, jj = queries.shape
    tt = act_rot.shape[0]
    kc = (t1 - t0) * tk
    return pl.pallas_call(
        _lifted_kernel,
        grid=(t1 - t0,),
        in_specs=[
            pl.BlockSpec((tt, jj), lambda i: (0, 0)),
            pl.BlockSpec((tk, jj), lambda i: (t0 + i, 0)),
            pl.BlockSpec((nq, tk, jj), lambda i: (0, t0 + i, 0)),
        ],
        out_specs=pl.BlockSpec((nq, tt, tk), lambda i: (0, 0, i)),
        out_shape=jax.ShapeDtypeStruct((nq, tt, kc), F32),
        compiler_params=pltpu.CompilerParams(
            dimension_semantics=("arbitrary",), vmem_limit_bytes=48 * 1024 * 1024
        ),
        cost_estimate=pl.CostEstimate(
            flops=2 * nq * kc * jj * tt,
            bytes_accessed=(nq + 1) * kc * jj * 2 + nq * tt * kc * 4,
            transcendentals=0,
        ),
    )(act_rot, eigenvalues, queries)


def local(out_grads, in_acts, out_basis, in_basis, eigenvalues, queries, *, nr, nc, nl, ng):
    acts_all = _gather(in_acts, "row", nr, 0)
    grads_all = _gather_far_first(out_grads, "col", nc)
    act_part = jnp.dot(acts_all, in_basis, preferred_element_type=F32)
    nb = out_basis.shape[1] // 128
    cuts = [128 * round(i * nb / ng) for i in range(ng + 1)]
    grad_works = [
        (functools.partial(lambda g, c0, c1: jnp.dot(g, out_basis[:, c0:c1], preferred_element_type=F32), c0=c0, c1=c1), grads_all)
        for c0, c1 in zip(cuts[:-1], cuts[1:])
    ]
    grad_works[0] = grad_works[0] + (True,)
    act_rot, grad_parts = _allreduce_bf16(act_part, "col", nc, 1, grad_works, paths=0)
    grad_part = jnp.concatenate(grad_parts, axis=1)
    kk = queries.shape[1]
    tk = next(c for c in (512, 256, 128, kk) if kk % c == 0)
    nt = kk // tk
    weights = [2, 5, 2, 2, 2, 1] if nl == 6 else [1] * nl
    acc = [0]
    for w in weights:
        acc.append(acc[-1] + w)
    bounds = [round(a * nt / acc[-1]) for a in acc]
    spans = [(t0, t1) for t0, t1 in zip(bounds[:-1], bounds[1:]) if t1 > t0]
    works = [
        (functools.partial(lambda a, t0, t1: _lifted(a, eigenvalues, queries, t0, t1, tk), t0=t0, t1=t1), act_rot)
        for t0, t1 in spans
    ]
    grad_rot, lifted = _allreduce_bf16(grad_part, "row", nr, 1, works, paths=2)
    partial = None
    for (t0, t1), piece in zip(spans, lifted):
        g = grad_rot[:, t0 * tk : t1 * tk].astype(F32)
        term = jnp.sum(piece * g[None], axis=2)
        partial = term if partial is None else partial + term
    return _allreduce_small(_allreduce_small(partial, "col", nc), "row", nr)


def solution(mesh):
    in_specs = (
        P("col", "row"),
        P("row", "col"),
        P("row", "col"),
        P("col", "row"),
        P("col", "row"),
        P(None, "col", "row"),
    )
    fn = functools.partial(local, nr=mesh.shape["row"], nc=mesh.shape["col"], nl=6, ng=4)
    return jax.shard_map(fn, mesh=mesh, in_specs=in_specs, out_specs=P(), check_vma=False)
```

```python
import functools

import jax
import jax.numpy as jnp
from jax import lax
from jax.experimental import pallas as pl
from jax.experimental.pallas import tpu as pltpu
from jax.sharding import PartitionSpec as P

DAMPING = 0.1
F32 = jnp.float32
BF16 = jnp.bfloat16


def _swap(x, axis, n, b):
    return lax.ppermute(x, axis, [(i, i ^ b) for i in range(n)])


def _gather(x, axis, n, dim):
    me = lax.axis_index(axis)
    b = 1
    while b < n:
        other = _swap(x, axis, n, b)
        first = (me // b) % 2 == 0
        x = jnp.where(first, jnp.concatenate([x, other], dim), jnp.concatenate([other, x], dim))
        b *= 2
    return x


def _gather_far_first(x, axis, n):
    me = lax.axis_index(axis)
    y = x[None]
    b = n // 2
    while b >= 1:
        other = _swap(y, axis, n, b)
        first = (me // b) % 2 == 0
        lo = jnp.where(first, y, other)
        hi = jnp.where(first, other, y)
        y = jnp.stack([lo, hi], axis=1).reshape((2 * y.shape[0],) + x.shape)
        b //= 2
    return y.reshape((n * x.shape[0],) + x.shape[1:])


def _allreduce_bf16(x, axis, n, dim, works=(), paths=1):
    me = lax.axis_index(axis)
    bits = []
    b = 1
    while b < n:
        bits.append(b)
        b *= 2
    orders = [bits, bits[:1] + bits[:0:-1]][:paths]
    works = list(works)
    done = []

    def swap(vs, bs):
        work, arg, *free = works.pop(0) if works else (None, None)
        if work is None:
            return [_swap(v, axis, n, b) for v, b in zip(vs, bs)]
        if not free:
            *vs, arg = lax.optimization_barrier((*vs, arg))
        result = work(arg)
        others = [_swap(v, axis, n, b) for v, b in zip(vs, bs)]
        *others, result = lax.optimization_barrier((*others, result))
        done.append(result)
        return others

    w = x.shape[dim] // len(orders)
    xs = [lax.slice_in_dim(x, p * w, (p + 1) * w, axis=dim) for p in range(len(orders))]
    for r in range(len(bits)):
        keeps, sends = [], []
        for p, v in enumerate(xs):
            b = orders[p][r]
            half = v.shape[dim] // 2
            upper = (me // b) % 2 == 1
            lo = lax.slice_in_dim(v, 0, half, axis=dim)
            hi = lax.slice_in_dim(v, half, 2 * half, axis=dim)
            keeps.append(jnp.where(upper, hi, lo))
            sends.append(jnp.where(upper, lo, hi))
        others = swap(sends, [o[r] for o in orders])
        xs = [k + o for k, o in zip(keeps, others)]
    xs = [v.astype(BF16) for v in xs]
    for r in reversed(range(len(bits))):
        others = swap(xs, [o[r] for o in orders])
        new = []
        for p, (v, other) in enumerate(zip(xs, others)):
            first = (me // orders[p][r]) % 2 == 0
            new.append(jnp.where(first, jnp.concatenate([v, other], dim), jnp.concatenate([other, v], dim)))
        xs = new
    done += [w[0](w[1]) for w in works if w[0] is not None]
    return jnp.concatenate(xs, dim) if len(xs) > 1 else xs[0], done


def _allreduce_small(x, axis, n):
    b = 1
    while b < n:
        x = x + _swap(x, axis, n, b)
        b *= 2
    return x


def _lifted_kernel(a_ref, e_ref, q_ref, o_ref):
    recip = 1.0 / (e_ref[...].astype(F32) + DAMPING)
    a = a_ref[...]
    dims = (((1,), (1,)), ((), ()))
    for qi in range(q_ref.shape[0]):
        s = (q_ref[qi].astype(F32) * recip).astype(BF16)
        o_ref[qi] = lax.dot_general(a, s, dims, preferred_element_type=F32)


def _lifted(act_rot, eigenvalues, queries, t0, t1, tk):
    nq, kk, jj = queries.shape
    tt = act_rot.shape[0]
    kc = (t1 - t0) * tk
    return pl.pallas_call(
        _lifted_kernel,
        grid=(t1 - t0,),
        in_specs=[
            pl.BlockSpec((tt, jj), lambda i: (0, 0)),
            pl.BlockSpec((tk, jj), lambda i: (t0 + i, 0)),
            pl.BlockSpec((nq, tk, jj), lambda i: (0, t0 + i, 0)),
        ],
        out_specs=pl.BlockSpec((nq, tt, tk), lambda i: (0, 0, i)),
        out_shape=jax.ShapeDtypeStruct((nq, tt, kc), F32),
        compiler_params=pltpu.CompilerParams(
            dimension_semantics=("arbitrary",), vmem_limit_bytes=48 * 1024 * 1024
        ),
        cost_estimate=pl.CostEstimate(
            flops=2 * nq * kc * jj * tt,
            bytes_accessed=(nq + 1) * kc * jj * 2 + nq * tt * kc * 4,
            transcendentals=0,
        ),
    )(act_rot, eigenvalues, queries)


def local(out_grads, in_acts, out_basis, in_basis, eigenvalues, queries, *, nr, nc, nl, ng):
    acts_all = _gather(in_acts, "row", nr, 0)
    grads_all = _gather_far_first(out_grads, "col", nc)
    act_part = jnp.dot(acts_all, in_basis, preferred_element_type=F32)
    nb = out_basis.shape[1] // 128
    cuts = [128 * round(i * nb / ng) for i in range(ng + 1)]
    grad_works = [
        (functools.partial(lambda g, c0, c1: jnp.dot(g, out_basis[:, c0:c1], preferred_element_type=F32), c0=c0, c1=c1), grads_all)
        for c0, c1 in zip(cuts[:-1], cuts[1:])
    ]
    grad_works[0] = grad_works[0] + (True,)
    act_rot, grad_parts = _allreduce_bf16(act_part, "col", nc, 1, grad_works)
    grad_part = jnp.concatenate(grad_parts, axis=1)
    kk = queries.shape[1]
    tk = next(c for c in (512, 256, 128, kk) if kk % c == 0)
    nt = kk // tk
    weights = [2, 4, 2, 2, 2, 2] if nl == 6 else [1] * nl
    acc = [0]
    for w in weights:
        acc.append(acc[-1] + w)
    bounds = [round(a * nt / acc[-1]) for a in acc]
    spans = [(t0, t1) for t0, t1 in zip(bounds[:-1], bounds[1:]) if t1 > t0]
    works = [
        (functools.partial(lambda a, t0, t1: _lifted(a, eigenvalues, queries, t0, t1, tk), t0=t0, t1=t1), act_rot)
        for t0, t1 in spans
    ]
    grad_rot, lifted = _allreduce_bf16(grad_part, "row", nr, 1, works, paths=2)
    partial = None
    for (t0, t1), piece in zip(spans, lifted):
        g = grad_rot[:, t0 * tk : t1 * tk].astype(F32)
        term = jnp.sum(piece * g[None], axis=2)
        partial = term if partial is None else partial + term
    return _allreduce_small(_allreduce_small(partial, "col", nc), "row", nr)


def solution(mesh):
    in_specs = (
        P("col", "row"),
        P("row", "col"),
        P("row", "col"),
        P("col", "row"),
        P("col", "row"),
        P(None, "col", "row"),
    )
    fn = functools.partial(local, nr=mesh.shape["row"], nc=mesh.shape["col"], nl=6, ng=4)
    return jax.shard_map(fn, mesh=mesh, in_specs=in_specs, out_specs=P(), check_vma=False)
```

```python
import functools

import jax
import jax.numpy as jnp
from jax import lax
from jax.experimental import pallas as pl
from jax.experimental.pallas import tpu as pltpu
from jax.sharding import PartitionSpec as P

DAMPING = 0.1
F32 = jnp.float32
BF16 = jnp.bfloat16


def _swap(x, axis, n, b):
    return lax.ppermute(x, axis, [(i, i ^ b) for i in range(n)])


def _gather(x, axis, n, dim):
    me = lax.axis_index(axis)
    b = 1
    while b < n:
        other = _swap(x, axis, n, b)
        first = (me // b) % 2 == 0
        x = jnp.where(first, jnp.concatenate([x, other], dim), jnp.concatenate([other, x], dim))
        b *= 2
    return x


def _gather_far_first(x, axis, n):
    me = lax.axis_index(axis)
    y = x[None]
    b = n // 2
    while b >= 1:
        other = _swap(y, axis, n, b)
        first = (me // b) % 2 == 0
        lo = jnp.where(first, y, other)
        hi = jnp.where(first, other, y)
        y = jnp.stack([lo, hi], axis=1).reshape((2 * y.shape[0],) + x.shape)
        b //= 2
    return y.reshape((n * x.shape[0],) + x.shape[1:])


def _allreduce_bf16(x, axis, n, dim, works=(), paths=1):
    me = lax.axis_index(axis)
    bits = []
    b = 1
    while b < n:
        bits.append(b)
        b *= 2
    orders = [bits, bits[:1] + bits[:0:-1]][:paths]
    works = list(works)
    done = []

    def swap(vs, bs):
        work, arg, *free = works.pop(0) if works else (None, None)
        if work is None:
            return [_swap(v, axis, n, b) for v, b in zip(vs, bs)]
        if not free:
            *vs, arg = lax.optimization_barrier((*vs, arg))
        result = work(arg)
        others = [_swap(v, axis, n, b) for v, b in zip(vs, bs)]
        *others, result = lax.optimization_barrier((*others, result))
        done.append(result)
        return others

    w = x.shape[dim] // len(orders)
    xs = [lax.slice_in_dim(x, p * w, (p + 1) * w, axis=dim) for p in range(len(orders))]
    for r in range(len(bits)):
        keeps, sends = [], []
        for p, v in enumerate(xs):
            b = orders[p][r]
            half = v.shape[dim] // 2
            upper = (me // b) % 2 == 1
            lo = lax.slice_in_dim(v, 0, half, axis=dim)
            hi = lax.slice_in_dim(v, half, 2 * half, axis=dim)
            keeps.append(jnp.where(upper, hi, lo))
            sends.append(jnp.where(upper, lo, hi))
        others = swap(sends, [o[r] for o in orders])
        xs = [k + o for k, o in zip(keeps, others)]
    xs = [v.astype(BF16) for v in xs]
    for r in reversed(range(len(bits))):
        others = swap(xs, [o[r] for o in orders])
        new = []
        for p, (v, other) in enumerate(zip(xs, others)):
            first = (me // orders[p][r]) % 2 == 0
            new.append(jnp.where(first, jnp.concatenate([v, other], dim), jnp.concatenate([other, v], dim)))
        xs = new
    done += [w[0](w[1]) for w in works if w[0] is not None]
    return jnp.concatenate(xs, dim) if len(xs) > 1 else xs[0], done


def _allreduce_small(x, axis, n):
    b = 1
    while b < n:
        x = x + _swap(x, axis, n, b)
        b *= 2
    return x


def _lifted_kernel(a_ref, e_ref, q_ref, o_ref):
    recip = 1.0 / (e_ref[...].astype(F32) + DAMPING)
    a = a_ref[...]
    dims = (((1,), (1,)), ((), ()))
    for qi in range(q_ref.shape[0]):
        s = (q_ref[qi].astype(F32) * recip).astype(BF16)
        o_ref[qi] = lax.dot_general(a, s, dims, preferred_element_type=F32)


def _lifted(act_rot, eigenvalues, queries, t0, t1, tk):
    nq, kk, jj = queries.shape
    tt = act_rot.shape[0]
    kc = (t1 - t0) * tk
    return pl.pallas_call(
        _lifted_kernel,
        grid=(t1 - t0,),
        in_specs=[
            pl.BlockSpec((tt, jj), lambda i: (0, 0)),
            pl.BlockSpec((tk, jj), lambda i: (t0 + i, 0)),
            pl.BlockSpec((nq, tk, jj), lambda i: (0, t0 + i, 0)),
        ],
        out_specs=pl.BlockSpec((nq, tt, tk), lambda i: (0, 0, i)),
        out_shape=jax.ShapeDtypeStruct((nq, tt, kc), F32),
        compiler_params=pltpu.CompilerParams(
            dimension_semantics=("arbitrary",), vmem_limit_bytes=48 * 1024 * 1024
        ),
        cost_estimate=pl.CostEstimate(
            flops=2 * nq * kc * jj * tt,
            bytes_accessed=(nq + 1) * kc * jj * 2 + nq * tt * kc * 4,
            transcendentals=0,
        ),
    )(act_rot, eigenvalues, queries)


def local(out_grads, in_acts, out_basis, in_basis, eigenvalues, queries, *, nr, nc, nl, ng):
    acts_all = lax.all_gather(in_acts, "row", axis=0, tiled=True)
    grads_all = _gather_far_first(out_grads, "col", nc)
    act_part = jnp.dot(acts_all, in_basis, preferred_element_type=F32)
    nb = out_basis.shape[1] // 128
    cuts = [128 * round(i * nb / ng) for i in range(ng + 1)]
    grad_works = [
        (functools.partial(lambda g, c0, c1: jnp.dot(g, out_basis[:, c0:c1], preferred_element_type=F32), c0=c0, c1=c1), grads_all)
        for c0, c1 in zip(cuts[:-1], cuts[1:])
    ]
    grad_works[0] = grad_works[0] + (True,)
    act_rot, grad_parts = _allreduce_bf16(act_part, "col", nc, 1, grad_works)
    grad_part = jnp.concatenate(grad_parts, axis=1)
    kk = queries.shape[1]
    tk = next(c for c in (512, 256, 128, kk) if kk % c == 0)
    nt = kk // tk
    weights = [2, 4, 2, 2, 2, 2] if nl == 6 else [1] * nl
    acc = [0]
    for w in weights:
        acc.append(acc[-1] + w)
    bounds = [round(a * nt / acc[-1]) for a in acc]
    spans = [(t0, t1) for t0, t1 in zip(bounds[:-1], bounds[1:]) if t1 > t0]
    works = [
        (functools.partial(lambda a, t0, t1: _lifted(a, eigenvalues, queries, t0, t1, tk), t0=t0, t1=t1), act_rot)
        for t0, t1 in spans
    ]
    grad_rot, lifted = _allreduce_bf16(grad_part, "row", nr, 1, works, paths=2)
    partial = None
    for (t0, t1), piece in zip(spans, lifted):
        g = grad_rot[:, t0 * tk : t1 * tk].astype(F32)
        term = jnp.sum(piece * g[None], axis=2)
        partial = term if partial is None else partial + term
    return _allreduce_small(_allreduce_small(partial, "col", nc), "row", nr)


def solution(mesh):
    in_specs = (
        P("col", "row"),
        P("row", "col"),
        P("row", "col"),
        P("col", "row"),
        P("col", "row"),
        P(None, "col", "row"),
    )
    fn = functools.partial(local, nr=mesh.shape["row"], nc=mesh.shape["col"], nl=6, ng=4)
    return jax.shard_map(fn, mesh=mesh, in_specs=in_specs, out_specs=P(), check_vma=False)
```

```python
import functools

import jax
import jax.numpy as jnp
from jax import lax
from jax.experimental import pallas as pl
from jax.experimental.pallas import tpu as pltpu
from jax.sharding import PartitionSpec as P

DAMPING = 0.1
F32 = jnp.float32
BF16 = jnp.bfloat16


def _swap(x, axis, n, b):
    return lax.ppermute(x, axis, [(i, i ^ b) for i in range(n)])


def _gather(x, axis, n, dim):
    me = lax.axis_index(axis)
    b = 1
    while b < n:
        other = _swap(x, axis, n, b)
        first = (me // b) % 2 == 0
        x = jnp.where(first, jnp.concatenate([x, other], dim), jnp.concatenate([other, x], dim))
        b *= 2
    return x


def _gather_far_first(x, axis, n):
    me = lax.axis_index(axis)
    y = x[None]
    b = n // 2
    while b >= 1:
        other = _swap(y, axis, n, b)
        first = (me // b) % 2 == 0
        lo = jnp.where(first, y, other)
        hi = jnp.where(first, other, y)
        y = jnp.stack([lo, hi], axis=1).reshape((2 * y.shape[0],) + x.shape)
        b //= 2
    return y.reshape((n * x.shape[0],) + x.shape[1:])


def _allreduce_bf16(x, axis, n, dim, works=(), paths=1):
    me = lax.axis_index(axis)
    bits = []
    b = 1
    while b < n:
        bits.append(b)
        b *= 2
    orders = [bits, bits[:1] + bits[:0:-1]][:paths]
    works = list(works)
    done = []

    def swap(vs, bs):
        work, arg, *free = works.pop(0) if works else (None, None)
        if work is None:
            return [_swap(v, axis, n, b) for v, b in zip(vs, bs)]
        if not free:
            *vs, arg = lax.optimization_barrier((*vs, arg))
        result = work(arg)
        others = [_swap(v, axis, n, b) for v, b in zip(vs, bs)]
        *others, result = lax.optimization_barrier((*others, result))
        done.append(result)
        return others

    w = x.shape[dim] // len(orders)
    xs = [lax.slice_in_dim(x, p * w, (p + 1) * w, axis=dim) for p in range(len(orders))]
    for r in range(len(bits)):
        keeps, sends = [], []
        for p, v in enumerate(xs):
            b = orders[p][r]
            half = v.shape[dim] // 2
            upper = (me // b) % 2 == 1
            lo = lax.slice_in_dim(v, 0, half, axis=dim)
            hi = lax.slice_in_dim(v, half, 2 * half, axis=dim)
            keeps.append(jnp.where(upper, hi, lo))
            sends.append(jnp.where(upper, lo, hi))
        others = swap(sends, [o[r] for o in orders])
        xs = [k + o for k, o in zip(keeps, others)]
    xs = [v.astype(BF16) for v in xs]
    for r in reversed(range(len(bits))):
        others = swap(xs, [o[r] for o in orders])
        new = []
        for p, (v, other) in enumerate(zip(xs, others)):
            first = (me // orders[p][r]) % 2 == 0
            new.append(jnp.where(first, jnp.concatenate([v, other], dim), jnp.concatenate([other, v], dim)))
        xs = new
    done += [w[0](w[1]) for w in works if w[0] is not None]
    return jnp.concatenate(xs, dim) if len(xs) > 1 else xs[0], done


def _allreduce_small(x, axis, n):
    b = 1
    while b < n:
        x = x + _swap(x, axis, n, b)
        b *= 2
    return x


def _lifted_kernel(a_ref, e_ref, q_ref, o_ref):
    recip = 1.0 / (e_ref[...].astype(F32) + DAMPING)
    a = a_ref[...]
    dims = (((1,), (1,)), ((), ()))
    for qi in range(q_ref.shape[0]):
        s = (q_ref[qi].astype(F32) * recip).astype(BF16)
        o_ref[qi] = lax.dot_general(a, s, dims, preferred_element_type=F32)


def _lifted(act_rot, eigenvalues, queries, t0, t1, tk):
    nq, kk, jj = queries.shape
    tt = act_rot.shape[0]
    kc = (t1 - t0) * tk
    return pl.pallas_call(
        _lifted_kernel,
        grid=(t1 - t0,),
        in_specs=[
            pl.BlockSpec((tt, jj), lambda i: (0, 0)),
            pl.BlockSpec((tk, jj), lambda i: (t0 + i, 0)),
            pl.BlockSpec((nq, tk, jj), lambda i: (0, t0 + i, 0)),
        ],
        out_specs=pl.BlockSpec((nq, tt, tk), lambda i: (0, 0, i)),
        out_shape=jax.ShapeDtypeStruct((nq, tt, kc), F32),
        compiler_params=pltpu.CompilerParams(
            dimension_semantics=("arbitrary",), vmem_limit_bytes=48 * 1024 * 1024
        ),
        cost_estimate=pl.CostEstimate(
            flops=2 * nq * kc * jj * tt,
            bytes_accessed=(nq + 1) * kc * jj * 2 + nq * tt * kc * 4,
            transcendentals=0,
        ),
    )(act_rot, eigenvalues, queries)


def local(out_grads, in_acts, out_basis, in_basis, eigenvalues, queries, *, nr, nc, nl, ng):
    acts_all = _gather_far_first(in_acts, "row", nr)
    grads_all = _gather_far_first(out_grads, "col", nc)
    act_part = jnp.dot(acts_all, in_basis, preferred_element_type=F32)
    nb = out_basis.shape[1] // 128
    cuts = [128 * round(i * nb / ng) for i in range(ng + 1)]
    grad_works = [
        (functools.partial(lambda g, c0, c1: jnp.dot(g, out_basis[:, c0:c1], preferred_element_type=F32), c0=c0, c1=c1), grads_all)
        for c0, c1 in zip(cuts[:-1], cuts[1:])
    ]
    grad_works[0] = grad_works[0] + (True,)
    act_rot, grad_parts = _allreduce_bf16(act_part, "col", nc, 1, grad_works)
    grad_part = jnp.concatenate(grad_parts, axis=1)
    kk = queries.shape[1]
    tk = next(c for c in (512, 256, 128, kk) if kk % c == 0)
    nt = kk // tk
    weights = [2, 4, 2, 2, 2, 2] if nl == 6 else [1] * nl
    acc = [0]
    for w in weights:
        acc.append(acc[-1] + w)
    bounds = [round(a * nt / acc[-1]) for a in acc]
    spans = [(t0, t1) for t0, t1 in zip(bounds[:-1], bounds[1:]) if t1 > t0]
    works = [
        (functools.partial(lambda a, t0, t1: _lifted(a, eigenvalues, queries, t0, t1, tk), t0=t0, t1=t1), act_rot)
        for t0, t1 in spans
    ]
    grad_rot, lifted = _allreduce_bf16(grad_part, "row", nr, 1, works, paths=2)
    partial = None
    for (t0, t1), piece in zip(spans, lifted):
        g = grad_rot[:, t0 * tk : t1 * tk].astype(F32)
        term = jnp.sum(piece * g[None], axis=2)
        partial = term if partial is None else partial + term
    return _allreduce_small(_allreduce_small(partial, "col", nc), "row", nr)


def solution(mesh):
    in_specs = (
        P("col", "row"),
        P("row", "col"),
        P("row", "col"),
        P("col", "row"),
        P("col", "row"),
        P(None, "col", "row"),
    )
    fn = functools.partial(local, nr=mesh.shape["row"], nc=mesh.shape["col"], nl=6, ng=4)
    return jax.shard_map(fn, mesh=mesh, in_specs=in_specs, out_specs=P(), check_vma=False)
```

```python
import functools

import jax
import jax.numpy as jnp
from jax import lax
from jax.experimental import pallas as pl
from jax.experimental.pallas import tpu as pltpu
from jax.sharding import PartitionSpec as P

DAMPING = 0.1
F32 = jnp.float32
BF16 = jnp.bfloat16


def _swap(x, axis, n, b):
    return lax.ppermute(x, axis, [(i, i ^ b) for i in range(n)])


def _gather(x, axis, n, dim):
    me = lax.axis_index(axis)
    b = 1
    while b < n:
        other = _swap(x, axis, n, b)
        first = (me // b) % 2 == 0
        x = jnp.where(first, jnp.concatenate([x, other], dim), jnp.concatenate([other, x], dim))
        b *= 2
    return x


def _gather_far_first(x, axis, n):
    me = lax.axis_index(axis)
    y = x[None]
    b = n // 2
    while b >= 1:
        other = _swap(y, axis, n, b)
        first = (me // b) % 2 == 0
        lo = jnp.where(first, y, other)
        hi = jnp.where(first, other, y)
        y = jnp.stack([lo, hi], axis=1).reshape((2 * y.shape[0],) + x.shape)
        b //= 2
    return y.reshape((n * x.shape[0],) + x.shape[1:])


def _allreduce_bf16(x, axis, n, dim, works=(), paths=1):
    me = lax.axis_index(axis)
    bits = []
    b = 1
    while b < n:
        bits.append(b)
        b *= 2
    orders = [bits, bits[:1] + bits[:0:-1]][:paths]
    works = list(works)
    done = []

    def swap(vs, bs):
        work, arg, *free = works.pop(0) if works else (None, None)
        if work is None:
            return [_swap(v, axis, n, b) for v, b in zip(vs, bs)]
        if not free:
            *vs, arg = lax.optimization_barrier((*vs, arg))
        result = work(arg)
        others = [_swap(v, axis, n, b) for v, b in zip(vs, bs)]
        *others, result = lax.optimization_barrier((*others, result))
        done.append(result)
        return others

    w = x.shape[dim] // len(orders)
    xs = [lax.slice_in_dim(x, p * w, (p + 1) * w, axis=dim) for p in range(len(orders))]
    for r in range(len(bits)):
        keeps, sends = [], []
        for p, v in enumerate(xs):
            b = orders[p][r]
            half = v.shape[dim] // 2
            upper = (me // b) % 2 == 1
            lo = lax.slice_in_dim(v, 0, half, axis=dim)
            hi = lax.slice_in_dim(v, half, 2 * half, axis=dim)
            keeps.append(jnp.where(upper, hi, lo))
            sends.append(jnp.where(upper, lo, hi))
        others = swap(sends, [o[r] for o in orders])
        xs = [k + o for k, o in zip(keeps, others)]
    xs = [v.astype(BF16) for v in xs]
    for r in reversed(range(len(bits))):
        others = swap(xs, [o[r] for o in orders])
        new = []
        for p, (v, other) in enumerate(zip(xs, others)):
            first = (me // orders[p][r]) % 2 == 0
            new.append(jnp.where(first, jnp.concatenate([v, other], dim), jnp.concatenate([other, v], dim)))
        xs = new
    done += [w[0](w[1]) for w in works if w[0] is not None]
    return jnp.concatenate(xs, dim) if len(xs) > 1 else xs[0], done


def _allreduce_small(x, axis, n):
    b = 1
    while b < n:
        x = x + _swap(x, axis, n, b)
        b *= 2
    return x


def _lifted_kernel(a_ref, e_ref, q_ref, o_ref):
    recip = 1.0 / (e_ref[...].astype(F32) + DAMPING)
    a = a_ref[...]
    dims = (((1,), (1,)), ((), ()))
    for qi in range(q_ref.shape[0]):
        s = (q_ref[qi].astype(F32) * recip).astype(BF16)
        o_ref[qi] = lax.dot_general(a, s, dims, preferred_element_type=F32)


def _lifted(act_rot, eigenvalues, queries, t0, t1, tk):
    nq, kk, jj = queries.shape
    tt = act_rot.shape[0]
    kc = (t1 - t0) * tk
    return pl.pallas_call(
        _lifted_kernel,
        grid=(t1 - t0,),
        in_specs=[
            pl.BlockSpec((tt, jj), lambda i: (0, 0)),
            pl.BlockSpec((tk, jj), lambda i: (t0 + i, 0)),
            pl.BlockSpec((nq, tk, jj), lambda i: (0, t0 + i, 0)),
        ],
        out_specs=pl.BlockSpec((nq, tt, tk), lambda i: (0, 0, i)),
        out_shape=jax.ShapeDtypeStruct((nq, tt, kc), F32),
        compiler_params=pltpu.CompilerParams(
            dimension_semantics=("arbitrary",), vmem_limit_bytes=48 * 1024 * 1024
        ),
        cost_estimate=pl.CostEstimate(
            flops=2 * nq * kc * jj * tt,
            bytes_accessed=(nq + 1) * kc * jj * 2 + nq * tt * kc * 4,
            transcendentals=0,
        ),
    )(act_rot, eigenvalues, queries)


def local(out_grads, in_acts, out_basis, in_basis, eigenvalues, queries, *, nr, nc, nl, ng):
    acts_all = _gather_far_first(in_acts, "row", nr)
    grads_all = _gather_far_first(out_grads, "col", nc)
    act_part = jnp.dot(acts_all, in_basis, preferred_element_type=F32)
    nb = out_basis.shape[1] // 128
    cuts = [128 * round(i * nb / ng) for i in range(ng + 1)]
    grad_works = [
        (functools.partial(lambda g, c0, c1: jnp.dot(g, out_basis[:, c0:c1], preferred_element_type=F32), c0=c0, c1=c1), grads_all)
        for c0, c1 in zip(cuts[:-1], cuts[1:])
    ]
    grad_works[0] = grad_works[0] + (True,)
    act_rot, grad_parts = _allreduce_bf16(act_part, "col", nc, 1, grad_works)
    grad_part = jnp.concatenate(grad_parts, axis=1)
    kk = queries.shape[1]
    tk = next(c for c in (512, 256, 128, kk) if kk % c == 0)
    nt = kk // tk
    weights = [2, 4, 2, 2, 2, 2] if nl == 6 else [1] * nl
    acc = [0]
    for w in weights:
        acc.append(acc[-1] + w)
    bounds = [round(a * nt / acc[-1]) for a in acc]
    spans = [(t0, t1) for t0, t1 in zip(bounds[:-1], bounds[1:]) if t1 > t0]
    works = [
        (functools.partial(lambda a, t0, t1: _lifted(a, eigenvalues, queries, t0, t1, tk), t0=t0, t1=t1), act_rot)
        for t0, t1 in spans
    ]
    grad_rot, lifted = _allreduce_bf16(grad_part, "row", nr, 1, works, paths=2)
    partial = None
    for (t0, t1), piece in zip(spans, lifted):
        g = grad_rot[:, t0 * tk : t1 * tk].astype(F32)
        term = jnp.sum(piece * g[None], axis=2)
        partial = term if partial is None else partial + term
    return _allreduce_small(_allreduce_small(partial, "col", nc), "row", nr)


def solution(mesh):
    in_specs = (
        P("col", "row"),
        P("row", "col"),
        P("row", "col"),
        P("col", "row"),
        P("col", "row"),
        P(None, "col", "row"),
    )
    fn = functools.partial(local, nr=mesh.shape["row"], nc=mesh.shape["col"], nl=6, ng=3)
    return jax.shard_map(fn, mesh=mesh, in_specs=in_specs, out_specs=P(), check_vma=False)
```

```python
import functools

import jax
import jax.numpy as jnp
from jax import lax
from jax.experimental import pallas as pl
from jax.experimental.pallas import tpu as pltpu
from jax.sharding import PartitionSpec as P

DAMPING = 0.1
F32 = jnp.float32
BF16 = jnp.bfloat16


def _swap(x, axis, n, b):
    return lax.ppermute(x, axis, [(i, i ^ b) for i in range(n)])


def _gather(x, axis, n, dim):
    me = lax.axis_index(axis)
    b = 1
    while b < n:
        other = _swap(x, axis, n, b)
        first = (me // b) % 2 == 0
        x = jnp.where(first, jnp.concatenate([x, other], dim), jnp.concatenate([other, x], dim))
        b *= 2
    return x


def _gather_far_first(x, axis, n):
    me = lax.axis_index(axis)
    y = x[None]
    b = n // 2
    while b >= 1:
        other = _swap(y, axis, n, b)
        first = (me // b) % 2 == 0
        lo = jnp.where(first, y, other)
        hi = jnp.where(first, other, y)
        y = jnp.stack([lo, hi], axis=1).reshape((2 * y.shape[0],) + x.shape)
        b //= 2
    return y.reshape((n * x.shape[0],) + x.shape[1:])


def _allreduce_bf16(x, axis, n, dim, works=(), paths=1):
    me = lax.axis_index(axis)
    bits = []
    b = 1
    while b < n:
        bits.append(b)
        b *= 2
    orders = [bits, bits[:1] + bits[:0:-1]][:paths]
    works = list(works)
    done = []

    def swap(vs, bs):
        work, arg, *free = works.pop(0) if works else (None, None)
        if work is None:
            return [_swap(v, axis, n, b) for v, b in zip(vs, bs)]
        if not free:
            *vs, arg = lax.optimization_barrier((*vs, arg))
        result = work(arg)
        others = [_swap(v, axis, n, b) for v, b in zip(vs, bs)]
        *others, result = lax.optimization_barrier((*others, result))
        done.append(result)
        return others

    w = x.shape[dim] // len(orders)
    xs = [lax.slice_in_dim(x, p * w, (p + 1) * w, axis=dim) for p in range(len(orders))]
    for r in range(len(bits)):
        keeps, sends = [], []
        for p, v in enumerate(xs):
            b = orders[p][r]
            half = v.shape[dim] // 2
            upper = (me // b) % 2 == 1
            lo = lax.slice_in_dim(v, 0, half, axis=dim)
            hi = lax.slice_in_dim(v, half, 2 * half, axis=dim)
            keeps.append(jnp.where(upper, hi, lo))
            sends.append(jnp.where(upper, lo, hi))
        others = swap(sends, [o[r] for o in orders])
        xs = [k + o for k, o in zip(keeps, others)]
    xs = [v.astype(BF16) for v in xs]
    for r in reversed(range(len(bits))):
        others = swap(xs, [o[r] for o in orders])
        new = []
        for p, (v, other) in enumerate(zip(xs, others)):
            first = (me // orders[p][r]) % 2 == 0
            new.append(jnp.where(first, jnp.concatenate([v, other], dim), jnp.concatenate([other, v], dim)))
        xs = new
    done += [w[0](w[1]) for w in works if w[0] is not None]
    return jnp.concatenate(xs, dim) if len(xs) > 1 else xs[0], done


def _allreduce_small(x, axis, n):
    b = 1
    while b < n:
        x = x + _swap(x, axis, n, b)
        b *= 2
    return x


def _lifted_kernel(a_ref, e_ref, q_ref, o_ref):
    recip = 1.0 / (e_ref[...].astype(F32) + DAMPING)
    a = a_ref[...]
    dims = (((1,), (1,)), ((), ()))
    for qi in range(q_ref.shape[0]):
        s = (q_ref[qi].astype(F32) * recip).astype(BF16)
        o_ref[qi] = lax.dot_general(a, s, dims, preferred_element_type=F32)


def _lifted(act_rot, eigenvalues, queries, t0, t1, tk):
    nq, kk, jj = queries.shape
    tt = act_rot.shape[0]
    kc = (t1 - t0) * tk
    return pl.pallas_call(
        _lifted_kernel,
        grid=(t1 - t0,),
        in_specs=[
            pl.BlockSpec((tt, jj), lambda i: (0, 0)),
            pl.BlockSpec((tk, jj), lambda i: (t0 + i, 0)),
            pl.BlockSpec((nq, tk, jj), lambda i: (0, t0 + i, 0)),
        ],
        out_specs=pl.BlockSpec((nq, tt, tk), lambda i: (0, 0, i)),
        out_shape=jax.ShapeDtypeStruct((nq, tt, kc), F32),
        compiler_params=pltpu.CompilerParams(
            dimension_semantics=("arbitrary",), vmem_limit_bytes=48 * 1024 * 1024
        ),
        cost_estimate=pl.CostEstimate(
            flops=2 * nq * kc * jj * tt,
            bytes_accessed=(nq + 1) * kc * jj * 2 + nq * tt * kc * 4,
            transcendentals=0,
        ),
    )(act_rot, eigenvalues, queries)


def local(out_grads, in_acts, out_basis, in_basis, eigenvalues, queries, *, nr, nc, nl, ng):
    acts_all = _gather_far_first(in_acts, "row", nr)
    grads_all = _gather_far_first(out_grads, "col", nc)
    act_part = jnp.dot(acts_all, in_basis, preferred_element_type=F32)
    nb = out_basis.shape[1] // 128
    cuts = [128 * round(i * nb / ng) for i in range(ng + 1)]
    grad_works = [
        (functools.partial(lambda g, c0, c1: jnp.dot(g, out_basis[:, c0:c1], preferred_element_type=F32), c0=c0, c1=c1), grads_all)
        for c0, c1 in zip(cuts[:-1], cuts[1:])
    ]
    grad_works[0] = grad_works[0] + (True,)
    act_rot, grad_parts = _allreduce_bf16(act_part, "col", nc, 1, grad_works)
    grad_part = jnp.concatenate(grad_parts, axis=1)
    kk = queries.shape[1]
    tk = next(c for c in (512, 256, 128, kk) if kk % c == 0)
    nt = kk // tk
    weights = [2, 4, 2, 2, 2, 2] if nl == 6 else [1] * nl
    acc = [0]
    for w in weights:
        acc.append(acc[-1] + w)
    bounds = [round(a * nt / acc[-1]) for a in acc]
    spans = [(t0, t1) for t0, t1 in zip(bounds[:-1], bounds[1:]) if t1 > t0]
    works = [
        (functools.partial(lambda a, t0, t1: _lifted(a, eigenvalues, queries, t0, t1, tk), t0=t0, t1=t1), act_rot)
        for t0, t1 in spans
    ]
    grad_rot, lifted = _allreduce_bf16(grad_part, "row", nr, 1, works, paths=2)
    partial = None
    for (t0, t1), piece in zip(spans, lifted):
        g = grad_rot[:, t0 * tk : t1 * tk].astype(F32)
        term = jnp.sum(piece * g[None], axis=2)
        partial = term if partial is None else partial + term
    return _allreduce_small(_allreduce_small(partial, "row", nr), "col", nc)


def solution(mesh):
    in_specs = (
        P("col", "row"),
        P("row", "col"),
        P("row", "col"),
        P("col", "row"),
        P("col", "row"),
        P(None, "col", "row"),
    )
    fn = functools.partial(local, nr=mesh.shape["row"], nc=mesh.shape["col"], nl=6, ng=4)
    return jax.shard_map(fn, mesh=mesh, in_specs=in_specs, out_specs=P(), check_vma=False)
```
